32 devices in a mesh: tensor: 4 (over y, x), context: 2 (over core), dp: 4 (over z).
Axes of the slice: x: 2, y: 2, z: 4, core: 2. Of those that a mesh axis runs over, the one named last changes fastest.
Arguments:
- q_pre: bfloat16 [4, 2, 128, 2048], P('dp', 'context', None, 'tensor'), may hold values from -6 to 6
- k_pre: bfloat16 [4, 2, 128, 256], P('dp', 'context'), may hold values from -6 to 6
- values: bfloat16 [4, 2, 128, 256], P('dp', 'context'), may hold values from -6 to 6
- cotangent: bfloat16 [4, 2, 128, 4096], P('dp', 'context', 'tensor'), may hold values from -6 to 6
- out_weight: bfloat16 [2048, 4096], P('tensor'), may hold values from -0.125 to 0.125
- q_gain: float32 [128], replicated, may hold values from 0.5 to 6
- k_gain: float32 [128], replicated, may hold values from 0.5 to 6
- block_position: int32 [4, 2], P('dp'), may hold values from 0 to 1, each once within a row
Outputs:
- d_queries: bfloat16 [4, 2, 128, 2048], P('dp', 'context', None, 'tensor')
- d_keys: bfloat16 [4, 2, 128, 256], P('dp', 'context', None, 'tensor')
- d_values: bfloat16 [4, 2, 128, 256], P('dp', 'context', None, 'tensor')
- d_q_gain: float32 [128], replicated
- d_k_gain: float32 [128], replicated
The draws below stay inside these ranges and needn't reach their ends.
Inputs may be any that keep to these rules, and one draw needn't show every extreme that they name: Each row of block_position is a permutation of the 2 blocks.
All inputs are finite; a program needn't handle non-finite values.
Results may differ from the reference program's by a relative error of at most 0.007.
The reference program's roundings to bfloat16 on the way count: a program that leaves them out, or rounds other values in their place, can miss the bound.
Values may be sent and summed in bfloat16 or wider, within the bound.
No kernel may reach another device: no remote copies, remote signals or barrier semaphores. Data moves between devices by JAX's collectives and lax.ppermute only.
A program may use at most 64 MiB of HBM per device.

```python
import math
import jax
import jax.numpy as jnp
from jax import lax

HD = 128
DW = 4096
BLK = 128
QHEADS = 16
KV_HEADS = 2
NBLK = 2
SEQS = 4


def shaped_keys(key):
    sample = jax.random.normal(jax.random.fold_in(key, 32), (SEQS, NBLK, BLK, KV_HEADS, HD), jnp.float32)
    return jnp.clip(sample, -6.0, 6.0)


def draw_k_pre(key, part):
    return shaped_keys(key).reshape(SEQS, NBLK, BLK, KV_HEADS * HD).astype(jnp.bfloat16)


def draw_q_pre(key, part):
    group_size = QHEADS // KV_HEADS
    sample = jax.random.normal(jax.random.fold_in(key, 34), (SEQS, NBLK, BLK, KV_HEADS, group_size, HD), jnp.float32)
    sample = jnp.clip(sample, -6.0, 6.0)
    return sample.reshape(SEQS, NBLK, BLK, QHEADS * HD).astype(jnp.bfloat16)


def draw_gain(key, salt):
    return jax.random.uniform(jax.random.fold_in(key, salt), (HD,), jnp.float32, 0.5, 1.5)


def draw_q_gain(key, part):
    return draw_gain(key, 41)


def draw_k_gain(key, part):
    return draw_gain(key, 42)


def block_levels(stream_key, extent, pieces, smallest, high):
    def one(axis_at, parts):
        draws = jax.random.uniform(jax.random.fold_in(jax.random.fold_in(stream_key, 6), axis_at), (parts,), jnp.float32, smallest / len(pieces), high / len(pieces))
        return jnp.repeat(jnp.exp(draws), extent[axis_at] // parts).reshape((-1,) + (1,) * (len(extent) - axis_at - 1))

    level = one(*pieces[0])
    for cut in pieces[1:]:
        level = level * one(*cut)
    return level


def normal_values(key, dims, width, reach, split=(), held_as=jnp.bfloat16):
    entries = jax.random.normal(key, dims, jnp.float32) * width
    if len(split) > 0:
        entries = block_levels(key, dims, split, -0.22, 0.18) * entries
    return jnp.clip(entries, min=-reach, max=reach).astype(held_as)


def setup_inputs(seed: int = 0) -> dict:
    seeds = jax.random.split(jax.random.key(seed), 9)
    q_pre = draw_q_pre(jax.random.fold_in(seeds[8], 71), 0)
    k_pre = draw_k_pre(jax.random.fold_in(seeds[8], 71), 0)
    values = normal_values(seeds[2], (SEQS, NBLK, BLK, KV_HEADS * HD), 1.0, 6.0, ((0, 4), (1, 2)))
    cotangent = normal_values(seeds[3], (SEQS, NBLK, BLK, DW), 1.0, 6.0, ((0, 4), (1, 2), (2, 4)))
    out_weight = normal_values(seeds[4], (QHEADS * HD, DW), (QHEADS * HD) ** -0.5, 0.125, ((0, 4),))
    q_gain = draw_q_gain(jax.random.fold_in(seeds[8], 71), 0)
    k_gain = draw_k_gain(jax.random.fold_in(seeds[8], 71), 0)
    block_position = jax.vmap(lambda own: jax.random.permutation(own, NBLK))(jax.random.split(seeds[7], SEQS)).reshape((SEQS, NBLK)).astype(jnp.int32)
    return dict(q_pre=q_pre, k_pre=k_pre, values=values, cotangent=cotangent, out_weight=out_weight, q_gain=q_gain, k_gain=k_gain, block_position=block_position)


EPS = 1e-06

def normalize(rows_in):
    inverse = lax.rsqrt(lax.optimization_barrier(jnp.mean(rows_in * rows_in, axis=-1, keepdims=True)) + EPS)
    return (rows_in * inverse, inverse)

def norm_backward(grad_norm, unit_rows, inverse, gain):
    scaled = grad_norm * gain
    return inverse * (scaled - unit_rows * lax.optimization_barrier(jnp.mean(scaled * unit_rows, axis=-1, keepdims=True)))

def lowered(values_in):
    return lax.optimization_barrier(values_in.astype(jnp.bfloat16)).astype(jnp.float32)

def group_backward(query_norm, key_norm, value_rows, grad_attn, visible):
    score_scale = 1.0 / math.sqrt(query_norm.shape[-1])
    precision_mode = lax.Precision.HIGHEST
    scores = jnp.einsum('hqd,kd->hqk', query_norm, key_norm, precision=precision_mode) * score_scale
    scores = jnp.where(visible[None], scores, -jnp.inf)
    row_max = lax.optimization_barrier(jnp.max(scores, axis=-1, keepdims=True))
    exponent = jnp.exp(scores - row_max)
    probabilities = exponent / lax.optimization_barrier(jnp.sum(exponent, axis=-1, keepdims=True))
    grad_prob = jnp.einsum('hqd,kd->hqk', grad_attn, value_rows, precision=precision_mode)
    row_delta = lax.optimization_barrier(jnp.sum(probabilities * grad_prob, axis=-1, keepdims=True))
    grad_score = lowered(probabilities * (grad_prob - row_delta) * score_scale)
    prob_low = lowered(probabilities)
    grad_query = jnp.einsum('hqk,kd->hqd', grad_score, key_norm, precision=precision_mode)
    grad_key = jnp.einsum('hqk,hqd->kd', grad_score, query_norm, precision=precision_mode)
    grad_value = jnp.einsum('hqk,hqd->kd', prob_low, grad_attn, precision=precision_mode)
    return (grad_query, grad_key, grad_value)

def reference(q_pre, k_pre, values, cotangent, out_weight, q_gain, k_gain, block_position):
    seq_count = q_pre.shape[0]
    length = NBLK * BLK
    group_size = QHEADS // KV_HEADS
    queries = q_pre.reshape(seq_count, length, QHEADS, HD).astype(jnp.float32)
    key_rows = k_pre.reshape(seq_count, length, KV_HEADS, HD).astype(jnp.float32)
    value_rows = values.reshape(seq_count, length, KV_HEADS, HD).astype(jnp.float32)
    grad_attn = jnp.dot(cotangent.reshape(seq_count * length, DW), out_weight.T, preferred_element_type=jnp.float32)
    grad_attn = lowered(grad_attn).reshape(seq_count, length, QHEADS, HD)
    offsets = jnp.arange(BLK, dtype=jnp.int32)
    positions = (block_position[:, :, None] * BLK + offsets[None, None, :]).reshape(seq_count, length)

    def one_sequence(sequence_item):
        query_seq, key_seq, value_seq, grad_seq, position_seq = sequence_item
        visible = position_seq[None, :] <= position_seq[:, None]
        query_unit, query_inverse = normalize(query_seq)
        key_unit, key_inverse = normalize(key_seq)
        query_norm = lowered(query_unit * q_gain)
        key_norm = lowered(key_unit * k_gain)
        query_groups = query_norm.reshape(length, KV_HEADS, group_size, HD).transpose(1, 2, 0, 3)
        grad_groups = grad_seq.reshape(length, KV_HEADS, group_size, HD).transpose(1, 2, 0, 3)

        def one_group(group_item):
            return group_backward(group_item[0], group_item[1], group_item[2], group_item[3], visible)
        grad_qn, grad_kn, grad_vs = lax.map(one_group, (query_groups, key_norm.transpose(1, 0, 2), value_seq.transpose(1, 0, 2), grad_groups))
        grad_qn = grad_qn.transpose(2, 0, 1, 3).reshape(length, QHEADS, HD)
        grad_kn = grad_kn.transpose(1, 0, 2)
        grad_vs = grad_vs.transpose(1, 0, 2)
        d_query = norm_backward(grad_qn, query_unit, query_inverse, q_gain)
        d_key = norm_backward(grad_kn, key_unit, key_inverse, k_gain)
        return (d_query.astype(jnp.bfloat16), d_key.astype(jnp.bfloat16), grad_vs.astype(jnp.bfloat16), lax.optimization_barrier(jnp.sum(grad_qn * query_unit, axis=(0, 1))), lax.optimization_barrier(jnp.sum(grad_kn * key_unit, axis=(0, 1))))
    d_queries, d_keys, d_values, gain_query, gain_key = lax.map(one_sequence, (queries, key_rows, value_rows, grad_attn, positions))
    return (d_queries.reshape(seq_count, NBLK, BLK, QHEADS * HD), d_keys.reshape(seq_count, NBLK, BLK, KV_HEADS * HD), d_values.reshape(seq_count, NBLK, BLK, KV_HEADS * HD), lax.optimization_barrier(jnp.sum(gain_query, axis=0)), lax.optimization_barrier(jnp.sum(gain_key, axis=0)))
```

```python
import math

import jax
import jax.numpy as jnp
from jax import lax
from jax.sharding import PartitionSpec as P

EPS = 1e-06


def xor_permute(value, axis, mask):
    size = lax.axis_size(axis)
    return lax.ppermute(value, axis, [(source, source ^ mask) for source in range(size)])


def normalize(rows_in):
    inverse = lax.rsqrt(jnp.mean(rows_in * rows_in, axis=-1, keepdims=True) + EPS)
    return (rows_in * inverse, inverse)


def norm_backward(grad_norm, unit_rows, inverse, gain):
    scaled = grad_norm * gain
    return inverse * (scaled - unit_rows * jnp.mean(scaled * unit_rows, axis=-1, keepdims=True))


def shards(q_pre, k_pre, values, cotangent, out_weight, q_gain, k_gain, block_position):
    tensor_count = lax.axis_size("tensor")
    context_count = lax.axis_size("context")
    dp_count = lax.axis_size("dp")
    for size in (tensor_count, context_count, dp_count):
        assert size & (size - 1) == 0
    tensor_pos = lax.axis_index("tensor")
    context_pos = lax.axis_index("context")
    head_size = q_gain.shape[0]
    block_rows = q_pre.shape[2]
    head_count = q_pre.shape[3] // head_size
    kv_count = k_pre.shape[3] // head_size
    per_kv = tensor_count // kv_count
    half_size = head_size // per_kv
    kv_column = tensor_pos // per_kv * head_size
    score_scale = 1.0 / math.sqrt(head_size)

    own_kv = jnp.concatenate(
        [
            lax.dynamic_slice_in_dim(k_pre[0, 0], kv_column, head_size, 1),
            lax.dynamic_slice_in_dim(values[0, 0], kv_column, head_size, 1),
        ],
        axis=1,
    )
    kv_slots = [own_kv] + [xor_permute(own_kv, "context", k) for k in range(1, context_count)]

    cot_own = cotangent[0, 0]
    cot_pieces = [cot_own] + [xor_permute(cot_own, "tensor", m) for m in range(1, tensor_count)]
    piece_rows = cot_own.shape[0]
    product = lax.dot_general(
        jnp.stack(cot_pieces, axis=0),
        out_weight,
        (((2,), (1,)), ((), ())),
        preferred_element_type=jnp.float32,
    ).astype(jnp.bfloat16)
    order = tensor_pos ^ jnp.arange(tensor_count, dtype=jnp.int32)
    grad_attn = jnp.take(product, order, axis=0).reshape(block_rows, head_count, head_size)

    offsets = jnp.arange(block_rows, dtype=jnp.int32)
    block_order = block_position[0]
    slot_blocks = jnp.take(block_order, context_pos ^ jnp.arange(context_count, dtype=jnp.int32))
    query_positions = slot_blocks[0] * block_rows + offsets
    key_positions = (slot_blocks[:, None] * block_rows + offsets[None, :]).reshape(-1)
    visible = key_positions[None, :] <= query_positions[:, None]

    query_unit, query_inverse = normalize(
        q_pre[0, 0].reshape(block_rows, head_count, head_size).astype(jnp.float32)
    )
    query_norm = (query_unit * q_gain).astype(jnp.bfloat16)
    kv_all = jnp.concatenate(kv_slots, axis=0)
    key_unit, key_inverse = normalize(kv_all[:, :head_size].astype(jnp.float32))
    key_norm = (key_unit * k_gain).astype(jnp.bfloat16)
    value_rows = kv_all[:, head_size:]

    scores = (
        jnp.einsum("qhd,kd->hqk", query_norm, key_norm, preferred_element_type=jnp.float32)
        * score_scale
    )
    scores = jnp.where(visible[None], scores, -jnp.inf)
    row_max = jnp.max(scores, axis=-1, keepdims=True)
    exponent = jnp.exp(scores - row_max)
    probs = exponent / jnp.sum(exponent, axis=-1, keepdims=True)
    grad_prob = jnp.einsum("qhd,kd->hqk", grad_attn, value_rows, preferred_element_type=jnp.float32)
    row_delta = jnp.sum(probs * grad_prob, axis=-1, keepdims=True)
    grad_score = (probs * (grad_prob - row_delta) * score_scale).astype(jnp.bfloat16)
    prob_low = probs.astype(jnp.bfloat16)
    grad_qn = jnp.einsum("hqk,kd->qhd", grad_score, key_norm, preferred_element_type=jnp.float32)
    key_part = jnp.einsum("hqk,qhd->kd", grad_score, query_norm, preferred_element_type=jnp.float32)
    value_part = jnp.einsum("hqk,qhd->kd", prob_low, grad_attn, preferred_element_type=jnp.float32)

    d_query = norm_backward(grad_qn, query_unit, query_inverse, q_gain).astype(jnp.bfloat16)
    gain_query_part = jnp.sum(grad_qn * query_unit, axis=(0, 1))
    gain_key_part = jnp.sum(key_part * key_unit, axis=0)

    gains = jnp.stack([gain_query_part, gain_key_part], axis=0)
    for axis, size in (("context", context_count), ("tensor", tensor_count), ("dp", dp_count)):
        bit = 1
        while bit < size:
            gains = gains + xor_permute(gains, axis, bit)
            bit *= 2

    key_slots = key_part.reshape(context_count, block_rows, head_size)
    value_slots = value_part.reshape(context_count, block_rows, head_size)
    half_index = tensor_pos % per_kv
    key_total = key_slots[0]
    value_total = lax.dynamic_slice_in_dim(value_slots[0], half_index * half_size, half_size, 1)
    group_size = tensor_count * context_count
    for m in range(per_kv):
        for k in range(context_count):
            if m == 0 and k == 0:
                continue
            target_half = (tensor_pos ^ m) % per_kv
            term = jnp.concatenate(
                [
                    key_slots[k],
                    lax.dynamic_slice_in_dim(value_slots[k], target_half * half_size, half_size, 1),
                ],
                axis=1,
            )
            pairs = []
            for source in range(group_size):
                st, sc = divmod(source, context_count)
                pairs.append((source, (st ^ m) * context_count + (sc ^ k)))
            arrived = lax.ppermute(term, ("tensor", "context"), pairs)
            key_total = key_total + arrived[:, :head_size]
            value_total = value_total + arrived[:, head_size:]

    own_unit = key_unit[:block_rows]
    own_inverse = key_inverse[:block_rows]
    d_key_full = norm_backward(key_total, own_unit, own_inverse, k_gain)
    d_key_half = lax.dynamic_slice_in_dim(d_key_full, half_index * half_size, half_size, 1)
    return (
        d_query.reshape(1, 1, block_rows, head_count * head_size),
        d_key_half.astype(jnp.bfloat16).reshape(1, 1, block_rows, half_size),
        value_total.astype(jnp.bfloat16).reshape(1, 1, block_rows, half_size),
        gains[0],
        gains[1],
    )


def solution(mesh):
    placed = (
        P("dp", "context", None, "tensor"),
        P("dp", "context", None, None),
        P("dp", "context", None, None),
        P("dp", "context", "tensor", None),
        P("tensor", None),
        P(),
        P(),
        P("dp", None),
    )
    return jax.shard_map(
        shards,
        mesh=mesh,
        in_specs=placed,
        out_specs=(
            P("dp", "context", None, "tensor"),
            P("dp", "context", None, "tensor"),
            P("dp", "context", None, "tensor"),
            P(),
            P(),
        ),
        check_vma=False,
    )
```

```python
import math

import jax
import jax.numpy as jnp
from jax import lax
from jax.sharding import PartitionSpec as P

EPS = 1e-06
MESH_AXES = ("tensor", "context", "dp")


def xor_permute(value, axis, mask):
    size = lax.axis_size(axis)
    return lax.ppermute(value, axis, [(source, source ^ mask) for source in range(size)])


def group_sum(value, bits):
    axes = tuple(axis for axis in MESH_AXES if any(axis == name for name, _ in bits))
    sizes = [lax.axis_size(axis) for axis in axes]
    position = 0
    for index, (axis, bit) in enumerate(bits):
        position = position + ((lax.axis_index(axis) & bit) != 0).astype(jnp.int32) * (1 << index)
    pieces = [value]
    for combo in range(1, 2 ** len(bits)):
        masks = [0] * len(axes)
        for index, (axis, bit) in enumerate(bits):
            if combo >> index & 1:
                masks[axes.index(axis)] |= bit
        pairs = []
        for source in range(math.prod(sizes)):
            coords, rest = [], source
            for size in reversed(sizes):
                coords.append(rest % size)
                rest //= size
            coords.reverse()
            target = 0
            for coord, size, mask in zip(coords, sizes, masks):
                target = target * size + (coord ^ mask)
            pairs.append((source, target))
        pieces.append(lax.ppermute(value, axes if len(axes) > 1 else axes[0], pairs))
    stacked = jnp.stack(pieces, axis=0)
    ordered = jnp.take(stacked, position ^ jnp.arange(len(pieces), dtype=jnp.int32), axis=0)
    total = ordered[0]
    for index in range(1, len(pieces)):
        total = total + ordered[index]
    return total


def normalize(rows_in):
    inverse = lax.rsqrt(jnp.mean(rows_in * rows_in, axis=-1, keepdims=True) + EPS)
    return (rows_in * inverse, inverse)


def norm_backward(grad_norm, unit_rows, inverse, gain):
    scaled = grad_norm * gain
    return inverse * (scaled - unit_rows * jnp.mean(scaled * unit_rows, axis=-1, keepdims=True))


def shards(q_pre, k_pre, values, cotangent, out_weight, q_gain, k_gain, block_position):
    tensor_count = lax.axis_size("tensor")
    context_count = lax.axis_size("context")
    dp_count = lax.axis_size("dp")
    for size in (tensor_count, context_count, dp_count):
        assert size & (size - 1) == 0
    tensor_pos = lax.axis_index("tensor")
    context_pos = lax.axis_index("context")
    head_size = q_gain.shape[0]
    block_rows = q_pre.shape[2]
    head_count = q_pre.shape[3] // head_size
    kv_count = k_pre.shape[3] // head_size
    per_kv = tensor_count // kv_count
    half_size = head_size // per_kv
    kv_column = tensor_pos // per_kv * head_size
    score_scale = 1.0 / math.sqrt(head_size)

    own_kv = jnp.concatenate(
        [
            lax.dynamic_slice_in_dim(k_pre[0, 0], kv_column, head_size, 1),
            lax.dynamic_slice_in_dim(values[0, 0], kv_column, head_size, 1),
        ],
        axis=1,
    )
    kv_slots = [own_kv] + [xor_permute(own_kv, "context", k) for k in range(1, context_count)]

    cot_own = cotangent[0, 0]
    cot_pieces = [cot_own] + [xor_permute(cot_own, "tensor", m) for m in range(1, tensor_count)]
    piece_rows = cot_own.shape[0]
    product = lax.dot_general(
        jnp.stack(cot_pieces, axis=0),
        out_weight,
        (((2,), (1,)), ((), ())),
        preferred_element_type=jnp.float32,
    ).astype(jnp.bfloat16)
    order = tensor_pos ^ jnp.arange(tensor_count, dtype=jnp.int32)
    grad_attn = jnp.take(product, order, axis=0).reshape(block_rows, head_count, head_size)

    offsets = jnp.arange(block_rows, dtype=jnp.int32)
    block_order = block_position[0]
    slot_blocks = jnp.take(block_order, context_pos ^ jnp.arange(context_count, dtype=jnp.int32))
    query_positions = slot_blocks[0] * block_rows + offsets
    key_positions = (slot_blocks[:, None] * block_rows + offsets[None, :]).reshape(-1)
    visible = key_positions[None, :] <= query_positions[:, None]

    query_unit, query_inverse = normalize(
        q_pre[0, 0].reshape(block_rows, head_count, head_size).astype(jnp.float32)
    )
    query_norm = (query_unit * q_gain).astype(jnp.bfloat16)
    kv_all = jnp.concatenate(kv_slots, axis=0)
    key_unit, key_inverse = normalize(kv_all[:, :head_size].astype(jnp.float32))
    key_norm = (key_unit * k_gain).astype(jnp.bfloat16)
    value_rows = kv_all[:, head_size:]

    scores = (
        jnp.einsum("qhd,kd->hqk", query_norm, key_norm, preferred_element_type=jnp.float32)
        * score_scale
    )
    scores = jnp.where(visible[None], scores, -jnp.inf)
    row_max = jnp.max(scores, axis=-1, keepdims=True)
    exponent = jnp.exp(scores - row_max)
    probs = exponent / jnp.sum(exponent, axis=-1, keepdims=True)
    grad_prob = jnp.einsum("qhd,kd->hqk", grad_attn, value_rows, preferred_element_type=jnp.float32)
    row_delta = jnp.sum(probs * grad_prob, axis=-1, keepdims=True)
    grad_score = (probs * (grad_prob - row_delta) * score_scale).astype(jnp.bfloat16)
    prob_low = probs.astype(jnp.bfloat16)
    grad_qn = jnp.einsum("hqk,kd->qhd", grad_score, key_norm, preferred_element_type=jnp.float32)
    key_part = jnp.einsum("hqk,qhd->kd", grad_score, query_norm, preferred_element_type=jnp.float32)
    value_part = jnp.einsum("hqk,qhd->kd", prob_low, grad_attn, preferred_element_type=jnp.float32)

    d_query = norm_backward(grad_qn, query_unit, query_inverse, q_gain).astype(jnp.bfloat16)
    gain_query_part = jnp.sum(grad_qn * query_unit, axis=(0, 1))
    gain_key_part = jnp.sum(key_part * key_unit, axis=0)

    gains = jnp.stack([gain_query_part, gain_key_part], axis=0)
    bits = []
    for axis, size in (("context", context_count), ("tensor", tensor_count), ("dp", dp_count)):
        bit = 1
        while bit < size:
            bits.append((axis, bit))
            bit *= 2
    for start in range(0, len(bits), 3):
        gains = group_sum(gains, bits[start : start + 3])

    key_slots = key_part.reshape(context_count, block_rows, head_size)
    value_slots = value_part.reshape(context_count, block_rows, head_size)
    half_index = tensor_pos % per_kv
    key_total = key_slots[0]
    value_total = lax.dynamic_slice_in_dim(value_slots[0], half_index * half_size, half_size, 1)
    group_size = tensor_count * context_count
    for m in range(per_kv):
        for k in range(context_count):
            if m == 0 and k == 0:
                continue
            target_half = (tensor_pos ^ m) % per_kv
            term = jnp.concatenate(
                [
                    key_slots[k],
                    lax.dynamic_slice_in_dim(value_slots[k], target_half * half_size, half_size, 1),
                ],
                axis=1,
            )
            pairs = []
            for source in range(group_size):
                st, sc = divmod(source, context_count)
                pairs.append((source, (st ^ m) * context_count + (sc ^ k)))
            arrived = lax.ppermute(term, ("tensor", "context"), pairs)
            key_total = key_total + arrived[:, :head_size]
            value_total = value_total + arrived[:, head_size:]

    own_unit = key_unit[:block_rows]
    own_inverse = key_inverse[:block_rows]
    d_key_full = norm_backward(key_total, own_unit, own_inverse, k_gain)
    d_key_half = lax.dynamic_slice_in_dim(d_key_full, half_index * half_size, half_size, 1)
    return (
        d_query.reshape(1, 1, block_rows, head_count * head_size),
        d_key_half.astype(jnp.bfloat16).reshape(1, 1, block_rows, half_size),
        value_total.astype(jnp.bfloat16).reshape(1, 1, block_rows, half_size),
        gains[0],
        gains[1],
    )


def solution(mesh):
    placed = (
        P("dp", "context", None, "tensor"),
        P("dp", "context", None, None),
        P("dp", "context", None, None),
        P("dp", "context", "tensor", None),
        P("tensor", None),
        P(),
        P(),
        P("dp", None),
    )
    return jax.shard_map(
        shards,
        mesh=mesh,
        in_specs=placed,
        out_specs=(
            P("dp", "context", None, "tensor"),
            P("dp", "context", None, "tensor"),
            P("dp", "context", None, "tensor"),
            P(),
            P(),
        ),
        check_vma=False,
    )
```

```python
import math

import jax
import jax.numpy as jnp
from jax import lax
from jax.sharding import PartitionSpec as P

EPS = 1e-06
MESH_AXES = ("tensor", "context", "dp")


def xor_permute(value, axis, mask):
    size = lax.axis_size(axis)
    return lax.ppermute(value, axis, [(source, source ^ mask) for source in range(size)])


def group_sum(value, bits):
    axes = tuple(axis for axis in MESH_AXES if any(axis == name for name, _ in bits))
    sizes = [lax.axis_size(axis) for axis in axes]
    position = 0
    for index, (axis, bit) in enumerate(bits):
        position = position + ((lax.axis_index(axis) & bit) != 0).astype(jnp.int32) * (1 << index)
    pieces = [value]
    for combo in range(1, 2 ** len(bits)):
        masks = [0] * len(axes)
        for index, (axis, bit) in enumerate(bits):
            if combo >> index & 1:
                masks[axes.index(axis)] |= bit
        pairs = []
        for source in range(math.prod(sizes)):
            coords, rest = [], source
            for size in reversed(sizes):
                coords.append(rest % size)
                rest //= size
            coords.reverse()
            target = 0
            for coord, size, mask in zip(coords, sizes, masks):
                target = target * size + (coord ^ mask)
            pairs.append((source, target))
        pieces.append(lax.ppermute(value, axes if len(axes) > 1 else axes[0], pairs))
    stacked = jnp.stack(pieces, axis=0)
    ordered = jnp.take(stacked, position ^ jnp.arange(len(pieces), dtype=jnp.int32), axis=0)
    total = ordered[0]
    for index in range(1, len(pieces)):
        total = total + ordered[index]
    return total


def all_sum(value):
    count = math.prod(lax.axis_size(axis) for axis in MESH_AXES)
    spread = jnp.broadcast_to(value[None], (count,) + value.shape)
    pieces = lax.all_to_all(spread, MESH_AXES, 0, 0, tiled=True)
    total = pieces[0]
    for index in range(1, count):
        total = total + pieces[index]
    return total


def normalize(rows_in):
    inverse = lax.rsqrt(jnp.mean(rows_in * rows_in, axis=-1, keepdims=True) + EPS)
    return (rows_in * inverse, inverse)


def norm_backward(grad_norm, unit_rows, inverse, gain):
    scaled = grad_norm * gain
    return inverse * (scaled - unit_rows * jnp.mean(scaled * unit_rows, axis=-1, keepdims=True))


def shards(q_pre, k_pre, values, cotangent, out_weight, q_gain, k_gain, block_position):
    tensor_count = lax.axis_size("tensor")
    context_count = lax.axis_size("context")
    dp_count = lax.axis_size("dp")
    for size in (tensor_count, context_count, dp_count):
        assert size & (size - 1) == 0
    tensor_pos = lax.axis_index("tensor")
    context_pos = lax.axis_index("context")
    head_size = q_gain.shape[0]
    block_rows = q_pre.shape[2]
    head_count = q_pre.shape[3] // head_size
    kv_count = k_pre.shape[3] // head_size
    per_kv = tensor_count // kv_count
    half_size = head_size // per_kv
    kv_column = tensor_pos // per_kv * head_size
    score_scale = 1.0 / math.sqrt(head_size)

    own_kv = jnp.concatenate(
        [
            lax.dynamic_slice_in_dim(k_pre[0, 0], kv_column, head_size, 1),
            lax.dynamic_slice_in_dim(values[0, 0], kv_column, head_size, 1),
        ],
        axis=1,
    )
    kv_slots = [own_kv] + [xor_permute(own_kv, "context", k) for k in range(1, context_count)]

    cot_own = cotangent[0, 0]
    cot_pieces = [cot_own] + [xor_permute(cot_own, "tensor", m) for m in range(1, tensor_count)]
    piece_rows = cot_own.shape[0]
    product = lax.dot_general(
        jnp.stack(cot_pieces, axis=0),
        out_weight,
        (((2,), (1,)), ((), ())),
        preferred_element_type=jnp.float32,
    ).astype(jnp.bfloat16)
    order = tensor_pos ^ jnp.arange(tensor_count, dtype=jnp.int32)
    grad_attn = jnp.take(product, order, axis=0).reshape(block_rows, head_count, head_size)

    offsets = jnp.arange(block_rows, dtype=jnp.int32)
    block_order = block_position[0]
    slot_blocks = jnp.take(block_order, context_pos ^ jnp.arange(context_count, dtype=jnp.int32))
    query_positions = slot_blocks[0] * block_rows + offsets
    key_positions = (slot_blocks[:, None] * block_rows + offsets[None, :]).reshape(-1)
    visible = key_positions[None, :] <= query_positions[:, None]

    query_unit, query_inverse = normalize(
        q_pre[0, 0].reshape(block_rows, head_count, head_size).astype(jnp.float32)
    )
    query_norm = (query_unit * q_gain).astype(jnp.bfloat16)
    kv_all = jnp.concatenate(kv_slots, axis=0)
    key_unit, key_inverse = normalize(kv_all[:, :head_size].astype(jnp.float32))
    key_norm = (key_unit * k_gain).astype(jnp.bfloat16)
    value_rows = kv_all[:, head_size:]

    scores = (
        jnp.einsum("qhd,kd->hqk", query_norm, key_norm, preferred_element_type=jnp.float32)
        * score_scale
    )
    scores = jnp.where(visible[None], scores, -jnp.inf)
    row_max = jnp.max(scores, axis=-1, keepdims=True)
    exponent = jnp.exp(scores - row_max)
    probs = exponent / jnp.sum(exponent, axis=-1, keepdims=True)
    grad_prob = jnp.einsum("qhd,kd->hqk", grad_attn, value_rows, preferred_element_type=jnp.float32)
    row_delta = jnp.sum(probs * grad_prob, axis=-1, keepdims=True)
    grad_score = (probs * (grad_prob - row_delta) * score_scale).astype(jnp.bfloat16)
    prob_low = probs.astype(jnp.bfloat16)
    grad_qn = jnp.einsum("hqk,kd->qhd", grad_score, key_norm, preferred_element_type=jnp.float32)
    key_part = jnp.einsum("hqk,qhd->kd", grad_score, query_norm, preferred_element_type=jnp.float32)
    value_part = jnp.einsum("hqk,qhd->kd", prob_low, grad_attn, preferred_element_type=jnp.float32)

    d_query = norm_backward(grad_qn, query_unit, query_inverse, q_gain).astype(jnp.bfloat16)
    gain_query_part = jnp.sum(grad_qn * query_unit, axis=(0, 1))
    gain_key_part = jnp.sum(key_part * key_unit, axis=0)

    gains = jnp.stack([gain_query_part, gain_key_part], axis=0)
    gains = all_sum(gains)

    key_slots = key_part.reshape(context_count, block_rows, head_size)
    value_slots = value_part.reshape(context_count, block_rows, head_size)
    half_index = tensor_pos % per_kv
    key_total = key_slots[0]
    value_total = lax.dynamic_slice_in_dim(value_slots[0], half_index * half_size, half_size, 1)
    group_size = tensor_count * context_count
    for m in range(per_kv):
        for k in range(context_count):
            if m == 0 and k == 0:
                continue
            target_half = (tensor_pos ^ m) % per_kv
            term = jnp.concatenate(
                [
                    key_slots[k],
                    lax.dynamic_slice_in_dim(value_slots[k], target_half * half_size, half_size, 1),
                ],
                axis=1,
            )
            pairs = []
            for source in range(group_size):
                st, sc = divmod(source, context_count)
                pairs.append((source, (st ^ m) * context_count + (sc ^ k)))
            arrived = lax.ppermute(term, ("tensor", "context"), pairs)
            key_total = key_total + arrived[:, :head_size]
            value_total = value_total + arrived[:, head_size:]

    own_unit = key_unit[:block_rows]
    own_inverse = key_inverse[:block_rows]
    d_key_full = norm_backward(key_total, own_unit, own_inverse, k_gain)
    d_key_half = lax.dynamic_slice_in_dim(d_key_full, half_index * half_size, half_size, 1)
    return (
        d_query.reshape(1, 1, block_rows, head_count * head_size),
        d_key_half.astype(jnp.bfloat16).reshape(1, 1, block_rows, half_size),
        value_total.astype(jnp.bfloat16).reshape(1, 1, block_rows, half_size),
        gains[0],
        gains[1],
    )


def solution(mesh):
    placed = (
        P("dp", "context", None, "tensor"),
        P("dp", "context", None, None),
        P("dp", "context", None, None),
        P("dp", "context", "tensor", None),
        P("tensor", None),
        P(),
        P(),
        P("dp", None),
    )
    return jax.shard_map(
        shards,
        mesh=mesh,
        in_specs=placed,
        out_specs=(
            P("dp", "context", None, "tensor"),
            P("dp", "context", None, "tensor"),
            P("dp", "context", None, "tensor"),
            P(),
            P(),
        ),
        check_vma=False,
    )
```

```python
import math

import jax
import jax.numpy as jnp
from jax import lax
from jax.sharding import PartitionSpec as P

EPS = 1e-06
MESH_AXES = ("tensor", "context", "dp")


def xor_permute(value, axis, mask):
    size = lax.axis_size(axis)
    return lax.ppermute(value, axis, [(source, source ^ mask) for source in range(size)])


def group_sum(value, bits):
    axes = tuple(axis for axis in MESH_AXES if any(axis == name for name, _ in bits))
    sizes = [lax.axis_size(axis) for axis in axes]
    position = 0
    for index, (axis, bit) in enumerate(bits):
        position = position + ((lax.axis_index(axis) & bit) != 0).astype(jnp.int32) * (1 << index)
    pieces = [value]
    for combo in range(1, 2 ** len(bits)):
        masks = [0] * len(axes)
        for index, (axis, bit) in enumerate(bits):
            if combo >> index & 1:
                masks[axes.index(axis)] |= bit
        pairs = []
        for source in range(math.prod(sizes)):
            coords, rest = [], source
            for size in reversed(sizes):
                coords.append(rest % size)
                rest //= size
            coords.reverse()
            target = 0
            for coord, size, mask in zip(coords, sizes, masks):
                target = target * size + (coord ^ mask)
            pairs.append((source, target))
        pieces.append(lax.ppermute(value, axes if len(axes) > 1 else axes[0], pairs))
    stacked = jnp.stack(pieces, axis=0)
    ordered = jnp.take(stacked, position ^ jnp.arange(len(pieces), dtype=jnp.int32), axis=0)
    total = ordered[0]
    for index in range(1, len(pieces)):
        total = total + ordered[index]
    return total


def all_sum(value):
    count = math.prod(lax.axis_size(axis) for axis in MESH_AXES)
    spread = jnp.broadcast_to(value[None], (count,) + value.shape)
    pieces = lax.all_to_all(spread, MESH_AXES, 0, 0, tiled=True)
    total = pieces[0]
    for index in range(1, count):
        total = total + pieces[index]
    return total


def normalize(rows_in):
    inverse = lax.rsqrt(jnp.mean(rows_in * rows_in, axis=-1, keepdims=True) + EPS)
    return (rows_in * inverse, inverse)


def norm_backward(grad_norm, unit_rows, inverse, gain):
    scaled = grad_norm * gain
    return inverse * (scaled - unit_rows * jnp.mean(scaled * unit_rows, axis=-1, keepdims=True))


def shards(q_pre, k_pre, values, cotangent, out_weight, q_gain, k_gain, block_position):
    tensor_count = lax.axis_size("tensor")
    context_count = lax.axis_size("context")
    dp_count = lax.axis_size("dp")
    for size in (tensor_count, context_count, dp_count):
        assert size & (size - 1) == 0
    tensor_pos = lax.axis_index("tensor")
    context_pos = lax.axis_index("context")
    head_size = q_gain.shape[0]
    block_rows = q_pre.shape[2]
    head_count = q_pre.shape[3] // head_size
    kv_count = k_pre.shape[3] // head_size
    per_kv = tensor_count // kv_count
    half_size = head_size // per_kv
    kv_column = tensor_pos // per_kv * head_size
    score_scale = 1.0 / math.sqrt(head_size)

    own_kv = jnp.concatenate(
        [
            lax.dynamic_slice_in_dim(k_pre[0, 0], kv_column, head_size, 1),
            lax.dynamic_slice_in_dim(values[0, 0], kv_column, head_size, 1),
        ],
        axis=1,
    )
    kv_slots = [own_kv] + [xor_permute(own_kv, "context", k) for k in range(1, context_count)]

    cot_own = cotangent[0, 0]
    piece_rows = cot_own.shape[0]
    cot_pieces = [cot_own] + [xor_permute(cot_own, "tensor", m) for m in range(1, tensor_count)]
    order = tensor_pos ^ jnp.arange(tensor_count, dtype=jnp.int32)

    offsets = jnp.arange(block_rows, dtype=jnp.int32)
    block_order = block_position[0]
    slot_blocks = jnp.take(block_order, context_pos ^ jnp.arange(context_count, dtype=jnp.int32))
    key_positions = (slot_blocks[:, None] * block_rows + offsets[None, :]).reshape(-1)

    query_rows = q_pre[0, 0].reshape(tensor_count, piece_rows, head_count, head_size)
    query_rows = jnp.take(query_rows, order, axis=0).astype(jnp.float32)
    query_unit, query_inverse = normalize(query_rows)
    query_norm = (query_unit * q_gain).astype(jnp.bfloat16)
    kv_all = jnp.concatenate(kv_slots, axis=0)
    key_unit, key_inverse = normalize(kv_all[:, :head_size].astype(jnp.float32))
    key_norm = (key_unit * k_gain).astype(jnp.bfloat16)
    value_rows = kv_all[:, head_size:]

    d_query_pieces = []
    key_part = None
    value_part = None
    gain_query_part = None
    for m in range(tensor_count):
        grad_attn = (
            lax.dot_general(
                cot_pieces[m],
                out_weight,
                (((1,), (1,)), ((), ())),
                preferred_element_type=jnp.float32,
            )
            .astype(jnp.bfloat16)
            .reshape(piece_rows, head_count, head_size)
        )
        piece_norm = query_norm[m]
        query_positions = (
            slot_blocks[0] * block_rows + order[m] * piece_rows + offsets[:piece_rows]
        )
        visible = key_positions[None, :] <= query_positions[:, None]
        scores = (
            jnp.einsum("qhd,kd->hqk", piece_norm, key_norm, preferred_element_type=jnp.float32)
            * score_scale
        )
        scores = jnp.where(visible[None], scores, -jnp.inf)
        row_max = jnp.max(scores, axis=-1, keepdims=True)
        exponent = jnp.exp(scores - row_max)
        probs = exponent / jnp.sum(exponent, axis=-1, keepdims=True)
        grad_prob = jnp.einsum(
            "qhd,kd->hqk", grad_attn, value_rows, preferred_element_type=jnp.float32
        )
        row_delta = jnp.sum(probs * grad_prob, axis=-1, keepdims=True)
        grad_score = (probs * (grad_prob - row_delta) * score_scale).astype(jnp.bfloat16)
        prob_low = probs.astype(jnp.bfloat16)
        grad_qn = jnp.einsum("hqk,kd->qhd", grad_score, key_norm, preferred_element_type=jnp.float32)
        key_term = jnp.einsum(
            "hqk,qhd->kd", grad_score, piece_norm, preferred_element_type=jnp.float32
        )
        value_term = jnp.einsum(
            "hqk,qhd->kd", prob_low, grad_attn, preferred_element_type=jnp.float32
        )
        gain_term = jnp.sum(grad_qn * query_unit[m], axis=(0, 1))
        d_query_pieces.append(
            norm_backward(grad_qn, query_unit[m], query_inverse[m], q_gain).astype(jnp.bfloat16)
        )
        if key_part is None:
            key_part, value_part, gain_query_part = key_term, value_term, gain_term
        else:
            key_part = key_part + key_term
            value_part = value_part + value_term
            gain_query_part = gain_query_part + gain_term
    d_query = jnp.take(jnp.stack(d_query_pieces, axis=0), order, axis=0)
    gain_key_part = jnp.sum(key_part * key_unit, axis=0)

    gains = jnp.stack([gain_query_part, gain_key_part], axis=0)
    gains = all_sum(gains)

    key_slots = key_part.reshape(context_count, block_rows, head_size)
    value_slots = value_part.reshape(context_count, block_rows, head_size)
    half_index = tensor_pos % per_kv
    key_total = key_slots[0]
    value_total = lax.dynamic_slice_in_dim(value_slots[0], half_index * half_size, half_size, 1)
    group_size = tensor_count * context_count
    for m in range(per_kv):
        for k in range(context_count):
            if m == 0 and k == 0:
                continue
            target_half = (tensor_pos ^ m) % per_kv
            term = jnp.concatenate(
                [
                    key_slots[k],
                    lax.dynamic_slice_in_dim(value_slots[k], target_half * half_size, half_size, 1),
                ],
                axis=1,
            )
            pairs = []
            for source in range(group_size):
                st, sc = divmod(source, context_count)
                pairs.append((source, (st ^ m) * context_count + (sc ^ k)))
            arrived = lax.ppermute(term, ("tensor", "context"), pairs)
            key_total = key_total + arrived[:, :head_size]
            value_total = value_total + arrived[:, head_size:]

    own_unit = key_unit[:block_rows]
    own_inverse = key_inverse[:block_rows]
    d_key_full = norm_backward(key_total, own_unit, own_inverse, k_gain)
    d_key_half = lax.dynamic_slice_in_dim(d_key_full, half_index * half_size, half_size, 1)
    return (
        d_query.reshape(1, 1, block_rows, head_count * head_size),
        d_key_half.astype(jnp.bfloat16).reshape(1, 1, block_rows, half_size),
        value_total.astype(jnp.bfloat16).reshape(1, 1, block_rows, half_size),
        gains[0],
        gains[1],
    )


def solution(mesh):
    placed = (
        P("dp", "context", None, "tensor"),
        P("dp", "context", None, None),
        P("dp", "context", None, None),
        P("dp", "context", "tensor", None),
        P("tensor", None),
        P(),
        P(),
        P("dp", None),
    )
    return jax.shard_map(
        shards,
        mesh=mesh,
        in_specs=placed,
        out_specs=(
            P("dp", "context", None, "tensor"),
            P("dp", "context", None, "tensor"),
            P("dp", "context", None, "tensor"),
            P(),
            P(),
        ),
        check_vma=False,
    )
```

```python
import math

import jax
import jax.numpy as jnp
from jax import lax
from jax.sharding import PartitionSpec as P
from jax.experimental import pallas as pl
from jax.experimental.pallas import tpu as pltpu

EPS = 1e-06
MESH_AXES = ("tensor", "context", "dp")


def xor_permute(value, axis, mask):
    size = lax.axis_size(axis)
    return lax.ppermute(value, axis, [(source, source ^ mask) for source in range(size)])


def group_sum(value, bits):
    axes = tuple(axis for axis in MESH_AXES if any(axis == name for name, _ in bits))
    sizes = [lax.axis_size(axis) for axis in axes]
    position = 0
    for index, (axis, bit) in enumerate(bits):
        position = position + ((lax.axis_index(axis) & bit) != 0).astype(jnp.int32) * (1 << index)
    pieces = [value]
    for combo in range(1, 2 ** len(bits)):
        masks = [0] * len(axes)
        for index, (axis, bit) in enumerate(bits):
            if combo >> index & 1:
                masks[axes.index(axis)] |= bit
        pairs = []
        for source in range(math.prod(sizes)):
            coords, rest = [], source
            for size in reversed(sizes):
                coords.append(rest % size)
                rest //= size
            coords.reverse()
            target = 0
            for coord, size, mask in zip(coords, sizes, masks):
                target = target * size + (coord ^ mask)
            pairs.append((source, target))
        pieces.append(lax.ppermute(value, axes if len(axes) > 1 else axes[0], pairs))
    stacked = jnp.stack(pieces, axis=0)
    ordered = jnp.take(stacked, position ^ jnp.arange(len(pieces), dtype=jnp.int32), axis=0)
    total = ordered[0]
    for index in range(1, len(pieces)):
        total = total + ordered[index]
    return total


def all_sum(value):
    count = math.prod(lax.axis_size(axis) for axis in MESH_AXES)
    spread = jnp.broadcast_to(value[None], (count,) + value.shape)
    pieces = lax.all_to_all(spread, MESH_AXES, 0, 0, tiled=True)
    total = pieces[0]
    for index in range(1, count):
        total = total + pieces[index]
    return total


def grad_attn_kernel(*refs):
    *cot_refs, weight_ref, out_ref, acc_ref = refs
    step = pl.program_id(0)

    @pl.when(step == 0)
    def _():
        acc_ref[...] = jnp.zeros_like(acc_ref)

    weight = weight_ref[...]
    for index, cot_ref in enumerate(cot_refs):
        acc_ref[index] += lax.dot_general(
            cot_ref[...], weight, (((1,), (1,)), ((), ())), preferred_element_type=jnp.float32
        )

    @pl.when(step == pl.num_programs(0) - 1)
    def _():
        out_ref[...] = acc_ref[...].astype(out_ref.dtype)


def grad_attn_matmul(pieces, weight, depth=1024):
    count, rows = len(pieces), pieces[0].shape[0]
    width, inner = weight.shape
    depth = min(depth, inner)
    return pl.pallas_call(
        grad_attn_kernel,
        out_shape=jax.ShapeDtypeStruct((count, rows, width), jnp.bfloat16),
        grid=(inner // depth,),
        in_specs=[pl.BlockSpec((rows, depth), lambda k: (0, k)) for _ in pieces]
        + [pl.BlockSpec((width, depth), lambda k: (0, k))],
        out_specs=pl.BlockSpec((count, rows, width), lambda k: (0, 0, 0)),
        scratch_shapes=[pltpu.VMEM((count, rows, width), jnp.float32)],
        compiler_params=pltpu.CompilerParams(dimension_semantics=("arbitrary",)),
        cost_estimate=pl.CostEstimate(
            flops=2 * count * rows * width * inner,
            bytes_accessed=2 * (count * rows * inner + width * inner + count * rows * width),
            transcendentals=0,
        ),
    )(*pieces, weight)


def normalize(rows_in):
    inverse = lax.rsqrt(jnp.mean(rows_in * rows_in, axis=-1, keepdims=True) + EPS)
    return (rows_in * inverse, inverse)


def norm_backward(grad_norm, unit_rows, inverse, gain):
    scaled = grad_norm * gain
    return inverse * (scaled - unit_rows * jnp.mean(scaled * unit_rows, axis=-1, keepdims=True))


def shards(q_pre, k_pre, values, cotangent, out_weight, q_gain, k_gain, block_position):
    tensor_count = lax.axis_size("tensor")
    context_count = lax.axis_size("context")
    dp_count = lax.axis_size("dp")
    for size in (tensor_count, context_count, dp_count):
        assert size & (size - 1) == 0
    tensor_pos = lax.axis_index("tensor")
    context_pos = lax.axis_index("context")
    head_size = q_gain.shape[0]
    block_rows = q_pre.shape[2]
    head_count = q_pre.shape[3] // head_size
    kv_count = k_pre.shape[3] // head_size
    per_kv = tensor_count // kv_count
    half_size = head_size // per_kv
    kv_column = tensor_pos // per_kv * head_size
    score_scale = 1.0 / math.sqrt(head_size)

    own_kv = jnp.concatenate(
        [
            lax.dynamic_slice_in_dim(k_pre[0, 0], kv_column, head_size, 1),
            lax.dynamic_slice_in_dim(values[0, 0], kv_column, head_size, 1),
        ],
        axis=1,
    )
    kv_slots = [own_kv] + [xor_permute(own_kv, "context", k) for k in range(1, context_count)]

    cot_own = cotangent[0, 0]
    cot_pieces = [cot_own] + [xor_permute(cot_own, "tensor", m) for m in range(1, tensor_count)]
    piece_rows = cot_own.shape[0]
    order = tensor_pos ^ jnp.arange(tensor_count, dtype=jnp.int32)
    grad_attn = grad_attn_matmul(cot_pieces, out_weight).reshape(block_rows, head_count, head_size)

    offsets = jnp.arange(block_rows, dtype=jnp.int32)
    block_order = block_position[0]
    slot_blocks = jnp.take(block_order, context_pos ^ jnp.arange(context_count, dtype=jnp.int32))
    query_positions = (
        slot_blocks[0] * block_rows + order[:, None] * piece_rows + offsets[None, :piece_rows]
    ).reshape(-1)
    key_positions = (slot_blocks[:, None] * block_rows + offsets[None, :]).reshape(-1)
    visible = key_positions[None, :] <= query_positions[:, None]

    query_rows = q_pre[0, 0].reshape(tensor_count, piece_rows, head_count, head_size)
    query_rows = jnp.take(query_rows, order, axis=0).reshape(block_rows, head_count, head_size)
    query_unit, query_inverse = normalize(query_rows.astype(jnp.float32))
    query_norm = (query_unit * q_gain).astype(jnp.bfloat16)
    kv_all = jnp.concatenate(kv_slots, axis=0)
    key_unit, key_inverse = normalize(kv_all[:, :head_size].astype(jnp.float32))
    key_norm = (key_unit * k_gain).astype(jnp.bfloat16)
    value_rows = kv_all[:, head_size:]

    scores = (
        jnp.einsum("qhd,kd->hqk", query_norm, key_norm, preferred_element_type=jnp.float32)
        * score_scale
    )
    scores = jnp.where(visible[None], scores, -jnp.inf)
    row_max = jnp.max(scores, axis=-1, keepdims=True)
    exponent = jnp.exp(scores - row_max)
    probs = exponent / jnp.sum(exponent, axis=-1, keepdims=True)
    grad_prob = jnp.einsum("qhd,kd->hqk", grad_attn, value_rows, preferred_element_type=jnp.float32)
    row_delta = jnp.sum(probs * grad_prob, axis=-1, keepdims=True)
    grad_score = (probs * (grad_prob - row_delta) * score_scale).astype(jnp.bfloat16)
    prob_low = probs.astype(jnp.bfloat16)
    grad_qn = jnp.einsum("hqk,kd->qhd", grad_score, key_norm, preferred_element_type=jnp.float32)
    key_part = jnp.einsum("hqk,qhd->kd", grad_score, query_norm, preferred_element_type=jnp.float32)
    value_part = jnp.einsum("hqk,qhd->kd", prob_low, grad_attn, preferred_element_type=jnp.float32)

    d_query = norm_backward(grad_qn, query_unit, query_inverse, q_gain).astype(jnp.bfloat16)
    d_query = jnp.take(d_query.reshape(tensor_count, piece_rows, -1), order, axis=0)
    gain_query_part = jnp.sum(grad_qn * query_unit, axis=(0, 1))
    gain_key_part = jnp.sum(key_part * key_unit, axis=0)

    gains = jnp.stack([gain_query_part, gain_key_part], axis=0)
    gains = all_sum(gains)

    key_slots = key_part.reshape(context_count, block_rows, head_size)
    value_slots = value_part.reshape(context_count, block_rows, head_size)
    half_index = tensor_pos % per_kv
    key_total = key_slots[0]
    value_total = lax.dynamic_slice_in_dim(value_slots[0], half_index * half_size, half_size, 1)
    group_size = tensor_count * context_count
    for m in range(per_kv):
        for k in range(context_count):
            if m == 0 and k == 0:
                continue
            target_half = (tensor_pos ^ m) % per_kv
            term = jnp.concatenate(
                [
                    key_slots[k],
                    lax.dynamic_slice_in_dim(value_slots[k], target_half * half_size, half_size, 1),
                ],
                axis=1,
            )
            pairs = []
            for source in range(group_size):
                st, sc = divmod(source, context_count)
                pairs.append((source, (st ^ m) * context_count + (sc ^ k)))
            arrived = lax.ppermute(term, ("tensor", "context"), pairs)
            key_total = key_total + arrived[:, :head_size]
            value_total = value_total + arrived[:, head_size:]

    own_unit = key_unit[:block_rows]
    own_inverse = key_inverse[:block_rows]
    d_key_full = norm_backward(key_total, own_unit, own_inverse, k_gain)
    d_key_half = lax.dynamic_slice_in_dim(d_key_full, half_index * half_size, half_size, 1)
    return (
        d_query.reshape(1, 1, block_rows, head_count * head_size),
        d_key_half.astype(jnp.bfloat16).reshape(1, 1, block_rows, half_size),
        value_total.astype(jnp.bfloat16).reshape(1, 1, block_rows, half_size),
        gains[0],
        gains[1],
    )


def solution(mesh):
    placed = (
        P("dp", "context", None, "tensor"),
        P("dp", "context", None, None),
        P("dp", "context", None, None),
        P("dp", "context", "tensor", None),
        P("tensor", None),
        P(),
        P(),
        P("dp", None),
    )
    return jax.shard_map(
        shards,
        mesh=mesh,
        in_specs=placed,
        out_specs=(
            P("dp", "context", None, "tensor"),
            P("dp", "context", None, "tensor"),
            P("dp", "context", None, "tensor"),
            P(),
            P(),
        ),
        check_vma=False,
    )
```

```python
import math

import jax
import jax.numpy as jnp
from jax import lax
from jax.sharding import PartitionSpec as P
from jax.experimental.layout import Layout, with_layout_constraint

EPS = 1e-06
MESH_AXES = ("tensor", "context", "dp")


def xor_permute(value, axis, mask):
    size = lax.axis_size(axis)
    return lax.ppermute(value, axis, [(source, source ^ mask) for source in range(size)])


def group_sum(value, bits):
    axes = tuple(axis for axis in MESH_AXES if any(axis == name for name, _ in bits))
    sizes = [lax.axis_size(axis) for axis in axes]
    position = 0
    for index, (axis, bit) in enumerate(bits):
        position = position + ((lax.axis_index(axis) & bit) != 0).astype(jnp.int32) * (1 << index)
    pieces = [value]
    for combo in range(1, 2 ** len(bits)):
        masks = [0] * len(axes)
        for index, (axis, bit) in enumerate(bits):
            if combo >> index & 1:
                masks[axes.index(axis)] |= bit
        pairs = []
        for source in range(math.prod(sizes)):
            coords, rest = [], source
            for size in reversed(sizes):
                coords.append(rest % size)
                rest //= size
            coords.reverse()
            target = 0
            for coord, size, mask in zip(coords, sizes, masks):
                target = target * size + (coord ^ mask)
            pairs.append((source, target))
        pieces.append(lax.ppermute(value, axes if len(axes) > 1 else axes[0], pairs))
    stacked = jnp.stack(pieces, axis=0)
    ordered = jnp.take(stacked, position ^ jnp.arange(len(pieces), dtype=jnp.int32), axis=0)
    total = ordered[0]
    for index in range(1, len(pieces)):
        total = total + ordered[index]
    return total


def all_sum(value):
    count = math.prod(lax.axis_size(axis) for axis in MESH_AXES)
    spread = jnp.broadcast_to(value[None], (count,) + value.shape)
    pieces = lax.all_to_all(spread, MESH_AXES, 0, 0, tiled=True)
    total = pieces[0]
    for index in range(1, count):
        total = total + pieces[index]
    return total


def normalize(rows_in):
    inverse = lax.rsqrt(jnp.mean(rows_in * rows_in, axis=-1, keepdims=True) + EPS)
    return (rows_in * inverse, inverse)


def norm_backward(grad_norm, unit_rows, inverse, gain):
    scaled = grad_norm * gain
    return inverse * (scaled - unit_rows * jnp.mean(scaled * unit_rows, axis=-1, keepdims=True))


def shards(q_pre, k_pre, values, cotangent, out_weight, q_gain, k_gain, block_position):
    tensor_count = lax.axis_size("tensor")
    context_count = lax.axis_size("context")
    dp_count = lax.axis_size("dp")
    for size in (tensor_count, context_count, dp_count):
        assert size & (size - 1) == 0
    tensor_pos = lax.axis_index("tensor")
    context_pos = lax.axis_index("context")
    head_size = q_gain.shape[0]
    block_rows = q_pre.shape[2]
    head_count = q_pre.shape[3] // head_size
    kv_count = k_pre.shape[3] // head_size
    per_kv = tensor_count // kv_count
    half_size = head_size // per_kv
    kv_column = tensor_pos // per_kv * head_size
    score_scale = 1.0 / math.sqrt(head_size)

    own_kv = jnp.concatenate(
        [
            lax.dynamic_slice_in_dim(k_pre[0, 0], kv_column, head_size, 1),
            lax.dynamic_slice_in_dim(values[0, 0], kv_column, head_size, 1),
        ],
        axis=1,
    )
    kv_slots = [own_kv] + [xor_permute(own_kv, "context", k) for k in range(1, context_count)]

    cot_own = cotangent[0, 0]
    cot_pieces = [cot_own] + [xor_permute(cot_own, "tensor", m) for m in range(1, tensor_count)]
    piece_rows = cot_own.shape[0]
    weight_t = with_layout_constraint(jnp.transpose(out_weight), Layout(major_to_minor=(0, 1)))
    product = lax.dot_general(
        jnp.stack(cot_pieces, axis=0),
        weight_t,
        (((2,), (0,)), ((), ())),
        preferred_element_type=jnp.float32,
    ).astype(jnp.bfloat16)
    order = tensor_pos ^ jnp.arange(tensor_count, dtype=jnp.int32)
    grad_attn = jnp.take(product, order, axis=0).reshape(block_rows, head_count, head_size)

    offsets = jnp.arange(block_rows, dtype=jnp.int32)
    block_order = block_position[0]
    slot_blocks = jnp.take(block_order, context_pos ^ jnp.arange(context_count, dtype=jnp.int32))
    query_positions = slot_blocks[0] * block_rows + offsets
    key_positions = (slot_blocks[:, None] * block_rows + offsets[None, :]).reshape(-1)
    visible = key_positions[None, :] <= query_positions[:, None]

    query_unit, query_inverse = normalize(
        q_pre[0, 0].reshape(block_rows, head_count, head_size).astype(jnp.float32)
    )
    query_norm = (query_unit * q_gain).astype(jnp.bfloat16)
    kv_all = jnp.concatenate(kv_slots, axis=0)
    key_unit, key_inverse = normalize(kv_all[:, :head_size].astype(jnp.float32))
    key_norm = (key_unit * k_gain).astype(jnp.bfloat16)
    value_rows = kv_all[:, head_size:]

    scores = (
        jnp.einsum("qhd,kd->hqk", query_norm, key_norm, preferred_element_type=jnp.float32)
        * score_scale
    )
    scores = jnp.where(visible[None], scores, -jnp.inf)
    row_max = jnp.max(scores, axis=-1, keepdims=True)
    exponent = jnp.exp(scores - row_max)
    probs = exponent / jnp.sum(exponent, axis=-1, keepdims=True)
    grad_prob = jnp.einsum("qhd,kd->hqk", grad_attn, value_rows, preferred_element_type=jnp.float32)
    row_delta = jnp.sum(probs * grad_prob, axis=-1, keepdims=True)
    grad_score = (probs * (grad_prob - row_delta) * score_scale).astype(jnp.bfloat16)
    prob_low = probs.astype(jnp.bfloat16)
    grad_qn = jnp.einsum("hqk,kd->qhd", grad_score, key_norm, preferred_element_type=jnp.float32)
    key_part = jnp.einsum("hqk,qhd->kd", grad_score, query_norm, preferred_element_type=jnp.float32)
    value_part = jnp.einsum("hqk,qhd->kd", prob_low, grad_attn, preferred_element_type=jnp.float32)

    d_query = norm_backward(grad_qn, query_unit, query_inverse, q_gain).astype(jnp.bfloat16)
    gain_query_part = jnp.sum(grad_qn * query_unit, axis=(0, 1))
    gain_key_part = jnp.sum(key_part * key_unit, axis=0)

    gains = jnp.stack([gain_query_part, gain_key_part], axis=0)
    gains = all_sum(gains)

    key_slots = key_part.reshape(context_count, block_rows, head_size)
    value_slots = value_part.reshape(context_count, block_rows, head_size)
    half_index = tensor_pos % per_kv
    key_total = key_slots[0]
    value_total = lax.dynamic_slice_in_dim(value_slots[0], half_index * half_size, half_size, 1)
    group_size = tensor_count * context_count
    for m in range(per_kv):
        for k in range(context_count):
            if m == 0 and k == 0:
                continue
            target_half = (tensor_pos ^ m) % per_kv
            term = jnp.concatenate(
                [
                    key_slots[k],
                    lax.dynamic_slice_in_dim(value_slots[k], target_half * half_size, half_size, 1),
                ],
                axis=1,
            )
            pairs = []
            for source in range(group_size):
                st, sc = divmod(source, context_count)
                pairs.append((source, (st ^ m) * context_count + (sc ^ k)))
            arrived = lax.ppermute(term, ("tensor", "context"), pairs)
            key_total = key_total + arrived[:, :head_size]
            value_total = value_total + arrived[:, head_size:]

    own_unit = key_unit[:block_rows]
    own_inverse = key_inverse[:block_rows]
    d_key_full = norm_backward(key_total, own_unit, own_inverse, k_gain)
    d_key_half = lax.dynamic_slice_in_dim(d_key_full, half_index * half_size, half_size, 1)
    return (
        d_query.reshape(1, 1, block_rows, head_count * head_size),
        d_key_half.astype(jnp.bfloat16).reshape(1, 1, block_rows, half_size),
        value_total.astype(jnp.bfloat16).reshape(1, 1, block_rows, half_size),
        gains[0],
        gains[1],
    )


def solution(mesh):
    placed = (
        P("dp", "context", None, "tensor"),
        P("dp", "context", None, None),
        P("dp", "context", None, None),
        P("dp", "context", "tensor", None),
        P("tensor", None),
        P(),
        P(),
        P("dp", None),
    )
    return jax.shard_map(
        shards,
        mesh=mesh,
        in_specs=placed,
        out_specs=(
            P("dp", "context", None, "tensor"),
            P("dp", "context", None, "tensor"),
            P("dp", "context", None, "tensor"),
            P(),
            P(),
        ),
        check_vma=False,
    )
```

```python
import math

import jax
import jax.numpy as jnp
from jax import lax
from jax.sharding import PartitionSpec as P
from jax.experimental.layout import Layout, with_layout_constraint

EPS = 1e-06
MESH_AXES = ("tensor", "context", "dp")
OUT_LAYOUT = Layout(major_to_minor=(0, 1, 3, 2))


def xor_permute(value, axis, mask):
    size = lax.axis_size(axis)
    return lax.ppermute(value, axis, [(source, source ^ mask) for source in range(size)])


def group_sum(value, bits):
    axes = tuple(axis for axis in MESH_AXES if any(axis == name for name, _ in bits))
    sizes = [lax.axis_size(axis) for axis in axes]
    position = 0
    for index, (axis, bit) in enumerate(bits):
        position = position + ((lax.axis_index(axis) & bit) != 0).astype(jnp.int32) * (1 << index)
    pieces = [value]
    for combo in range(1, 2 ** len(bits)):
        masks = [0] * len(axes)
        for index, (axis, bit) in enumerate(bits):
            if combo >> index & 1:
                masks[axes.index(axis)] |= bit
        pairs = []
        for source in range(math.prod(sizes)):
            coords, rest = [], source
            for size in reversed(sizes):
                coords.append(rest % size)
                rest //= size
            coords.reverse()
            target = 0
            for coord, size, mask in zip(coords, sizes, masks):
                target = target * size + (coord ^ mask)
            pairs.append((source, target))
        pieces.append(lax.ppermute(value, axes if len(axes) > 1 else axes[0], pairs))
    stacked = jnp.stack(pieces, axis=0)
    ordered = jnp.take(stacked, position ^ jnp.arange(len(pieces), dtype=jnp.int32), axis=0)
    total = ordered[0]
    for index in range(1, len(pieces)):
        total = total + ordered[index]
    return total


def all_sum(value):
    count = math.prod(lax.axis_size(axis) for axis in MESH_AXES)
    spread = jnp.broadcast_to(value[None], (count,) + value.shape)
    pieces = lax.all_to_all(spread, MESH_AXES, 0, 0, tiled=True)
    total = pieces[0]
    for index in range(1, count):
        total = total + pieces[index]
    return total


def normalize(rows_in):
    inverse = lax.rsqrt(jnp.mean(rows_in * rows_in, axis=-1, keepdims=True) + EPS)
    return (rows_in * inverse, inverse)


def norm_backward(grad_norm, unit_rows, inverse, gain):
    scaled = grad_norm * gain
    return inverse * (scaled - unit_rows * jnp.mean(scaled * unit_rows, axis=-1, keepdims=True))


def shards(q_pre, k_pre, values, cotangent, out_weight, q_gain, k_gain, block_position):
    tensor_count = lax.axis_size("tensor")
    context_count = lax.axis_size("context")
    dp_count = lax.axis_size("dp")
    for size in (tensor_count, context_count, dp_count):
        assert size & (size - 1) == 0
    tensor_pos = lax.axis_index("tensor")
    context_pos = lax.axis_index("context")
    head_size = q_gain.shape[0]
    block_rows = q_pre.shape[2]
    head_count = q_pre.shape[3] // head_size
    kv_count = k_pre.shape[3] // head_size
    per_kv = tensor_count // kv_count
    half_size = head_size // per_kv
    kv_column = tensor_pos // per_kv * head_size
    score_scale = 1.0 / math.sqrt(head_size)

    own_kv = jnp.concatenate(
        [
            lax.dynamic_slice_in_dim(k_pre[0, 0], kv_column, head_size, 1),
            lax.dynamic_slice_in_dim(values[0, 0], kv_column, head_size, 1),
        ],
        axis=1,
    )
    kv_slots = [own_kv] + [xor_permute(own_kv, "context", k) for k in range(1, context_count)]

    cot_own = cotangent[0, 0]
    cot_pieces = [cot_own] + [xor_permute(cot_own, "tensor", m) for m in range(1, tensor_count)]
    piece_rows = cot_own.shape[0]
    weight_t = with_layout_constraint(jnp.transpose(out_weight), Layout(major_to_minor=(0, 1)))
    product = lax.dot_general(
        jnp.stack(cot_pieces, axis=0),
        weight_t,
        (((2,), (0,)), ((), ())),
        preferred_element_type=jnp.float32,
    ).astype(jnp.bfloat16)
    order = tensor_pos ^ jnp.arange(tensor_count, dtype=jnp.int32)
    grad_attn = jnp.take(product, order, axis=0).reshape(block_rows, head_count, head_size)

    offsets = jnp.arange(block_rows, dtype=jnp.int32)
    block_order = block_position[0]
    slot_blocks = jnp.take(block_order, context_pos ^ jnp.arange(context_count, dtype=jnp.int32))
    query_positions = slot_blocks[0] * block_rows + offsets
    key_positions = (slot_blocks[:, None] * block_rows + offsets[None, :]).reshape(-1)
    visible = key_positions[None, :] <= query_positions[:, None]

    query_unit, query_inverse = normalize(
        q_pre[0, 0].reshape(block_rows, head_count, head_size).astype(jnp.float32)
    )
    query_norm = (query_unit * q_gain).astype(jnp.bfloat16)
    kv_all = jnp.concatenate(kv_slots, axis=0)
    key_unit, key_inverse = normalize(kv_all[:, :head_size].astype(jnp.float32))
    key_norm = (key_unit * k_gain).astype(jnp.bfloat16)
    value_rows = kv_all[:, head_size:]

    scores = (
        jnp.einsum("qhd,kd->hqk", query_norm, key_norm, preferred_element_type=jnp.float32)
        * score_scale
    )
    scores = jnp.where(visible[None], scores, -jnp.inf)
    row_max = jnp.max(scores, axis=-1, keepdims=True)
    exponent = jnp.exp(scores - row_max)
    probs = exponent / jnp.sum(exponent, axis=-1, keepdims=True)
    grad_prob = jnp.einsum("qhd,kd->hqk", grad_attn, value_rows, preferred_element_type=jnp.float32)
    row_delta = jnp.sum(probs * grad_prob, axis=-1, keepdims=True)
    grad_score = (probs * (grad_prob - row_delta) * score_scale).astype(jnp.bfloat16)
    prob_low = probs.astype(jnp.bfloat16)
    grad_qn = jnp.einsum("hqk,kd->qhd", grad_score, key_norm, preferred_element_type=jnp.float32)
    key_part = jnp.einsum("hqk,qhd->kd", grad_score, query_norm, preferred_element_type=jnp.float32)
    value_part = jnp.einsum("hqk,qhd->kd", prob_low, grad_attn, preferred_element_type=jnp.float32)

    d_query = norm_backward(grad_qn, query_unit, query_inverse, q_gain).astype(jnp.bfloat16)
    gain_query_part = jnp.sum(grad_qn * query_unit, axis=(0, 1))
    gain_key_part = jnp.sum(key_part * key_unit, axis=0)

    gains = jnp.stack([gain_query_part, gain_key_part], axis=0)
    gains = all_sum(gains)

    key_slots = key_part.reshape(context_count, block_rows, head_size)
    value_slots = value_part.reshape(context_count, block_rows, head_size)
    half_index = tensor_pos % per_kv
    key_total = key_slots[0]
    value_total = lax.dynamic_slice_in_dim(value_slots[0], half_index * half_size, half_size, 1)
    group_size = tensor_count * context_count
    for m in range(per_kv):
        for k in range(context_count):
            if m == 0 and k == 0:
                continue
            target_half = (tensor_pos ^ m) % per_kv
            term = jnp.concatenate(
                [
                    key_slots[k],
                    lax.dynamic_slice_in_dim(value_slots[k], target_half * half_size, half_size, 1),
                ],
                axis=1,
            )
            pairs = []
            for source in range(group_size):
                st, sc = divmod(source, context_count)
                pairs.append((source, (st ^ m) * context_count + (sc ^ k)))
            arrived = lax.ppermute(term, ("tensor", "context"), pairs)
            key_total = key_total + arrived[:, :head_size]
            value_total = value_total + arrived[:, head_size:]

    own_unit = key_unit[:block_rows]
    own_inverse = key_inverse[:block_rows]
    d_key_full = norm_backward(key_total, own_unit, own_inverse, k_gain)
    d_key_half = lax.dynamic_slice_in_dim(d_key_full, half_index * half_size, half_size, 1)
    return (
        d_query.reshape(1, 1, block_rows, head_count * head_size),
        with_layout_constraint(
            d_key_half.astype(jnp.bfloat16).reshape(1, 1, block_rows, half_size), OUT_LAYOUT
        ),
        with_layout_constraint(
            value_total.astype(jnp.bfloat16).reshape(1, 1, block_rows, half_size), OUT_LAYOUT
        ),
        gains[0],
        gains[1],
    )


def solution(mesh):
    placed = (
        P("dp", "context", None, "tensor"),
        P("dp", "context", None, None),
        P("dp", "context", None, None),
        P("dp", "context", "tensor", None),
        P("tensor", None),
        P(),
        P(),
        P("dp", None),
    )
    return jax.shard_map(
        shards,
        mesh=mesh,
        in_specs=placed,
        out_specs=(
            P("dp", "context", None, "tensor"),
            P("dp", "context", None, "tensor"),
            P("dp", "context", None, "tensor"),
            P(),
            P(),
        ),
        check_vma=False,
    )
```

```python
import math

import jax
import jax.numpy as jnp
from jax import lax
from jax.sharding import PartitionSpec as P
from jax.experimental import pallas as pl
from jax.experimental.pallas import tpu as pltpu
from jax.experimental.layout import Layout, with_layout_constraint

EPS = 1e-06
MESH_AXES = ("tensor", "context", "dp")
OUT_LAYOUT = Layout(major_to_minor=(0, 1, 3, 2))


def xor_permute(value, axis, mask):
    size = lax.axis_size(axis)
    return lax.ppermute(value, axis, [(source, source ^ mask) for source in range(size)])


def all_sum(value):
    count = math.prod(lax.axis_size(axis) for axis in MESH_AXES)
    spread = jnp.broadcast_to(value[None], (count,) + value.shape)
    pieces = lax.all_to_all(spread, MESH_AXES, 0, 0, tiled=True)
    total = pieces[0]
    for index in range(1, count):
        total = total + pieces[index]
    return total


def grad_attn_kernel(*refs):
    *cot_refs, weight_ref, out_ref, acc_ref = refs
    step = pl.program_id(0)

    @pl.when(step == 0)
    def _():
        acc_ref[...] = jnp.zeros_like(acc_ref)

    weight = weight_ref[...]
    rows = cot_refs[0].shape[0]
    if rows % 16 == 0:
        joined = jnp.concatenate([cot_ref[...] for cot_ref in cot_refs], axis=0)
        acc_ref[...] += jnp.dot(joined, weight, preferred_element_type=jnp.float32)
    else:
        for index, cot_ref in enumerate(cot_refs):
            acc_ref[pl.ds(index * rows, rows), :] += jnp.dot(
                cot_ref[...], weight, preferred_element_type=jnp.float32
            )

    @pl.when(step == pl.num_programs(0) - 1)
    def _():
        out_ref[...] = acc_ref[...].astype(out_ref.dtype)


def grad_attn_matmul(pieces, weight_t, depth=512):
    count, rows = len(pieces), pieces[0].shape[0]
    inner, width = weight_t.shape
    depth = min(depth, inner)
    return pl.pallas_call(
        grad_attn_kernel,
        out_shape=jax.ShapeDtypeStruct((count * rows, width), jnp.bfloat16),
        grid=(inner // depth,),
        in_specs=[pl.BlockSpec((rows, depth), lambda k: (0, k)) for _ in pieces]
        + [pl.BlockSpec((depth, width), lambda k: (k, 0))],
        out_specs=pl.BlockSpec((count * rows, width), lambda k: (0, 0)),
        scratch_shapes=[pltpu.VMEM((count * rows, width), jnp.float32)],
        compiler_params=pltpu.CompilerParams(dimension_semantics=("arbitrary",)),
        cost_estimate=pl.CostEstimate(
            flops=2 * count * rows * width * inner,
            bytes_accessed=2 * (count * rows * inner + width * inner + count * rows * width),
            transcendentals=0,
        ),
    )(*pieces, weight_t)


def normalize(rows_in):
    inverse = lax.rsqrt(jnp.mean(rows_in * rows_in, axis=-1, keepdims=True) + EPS)
    return (rows_in * inverse, inverse)


def norm_backward(grad_norm, unit_rows, inverse, gain):
    scaled = grad_norm * gain
    return inverse * (scaled - unit_rows * jnp.mean(scaled * unit_rows, axis=-1, keepdims=True))


def shard_body(q_pre, k_pre, values, cotangent, out_weight, q_gain, k_gain, block_position):
    tensor_count = lax.axis_size("tensor")
    context_count = lax.axis_size("context")
    dp_count = lax.axis_size("dp")
    for size in (tensor_count, context_count, dp_count):
        assert size & (size - 1) == 0
    tensor_pos = lax.axis_index("tensor")
    context_pos = lax.axis_index("context")
    head_size = q_gain.shape[0]
    block_rows = q_pre.shape[2]
    head_count = q_pre.shape[3] // head_size
    kv_count = k_pre.shape[3] // head_size
    per_kv = tensor_count // kv_count
    half_size = head_size // per_kv
    kv_column = tensor_pos // per_kv * head_size
    score_scale = 1.0 / math.sqrt(head_size)

    own_kv = jnp.concatenate(
        [
            lax.dynamic_slice_in_dim(k_pre[0, 0], kv_column, head_size, 1),
            lax.dynamic_slice_in_dim(values[0, 0], kv_column, head_size, 1),
        ],
        axis=1,
    )
    kv_slots = [own_kv] + [xor_permute(own_kv, "context", k) for k in range(1, context_count)]

    cot_own = cotangent[0, 0]
    cot_pieces = [cot_own] + [xor_permute(cot_own, "tensor", m) for m in range(1, tensor_count)]
    piece_rows = cot_own.shape[0]
    weight_t = with_layout_constraint(jnp.transpose(out_weight), Layout(major_to_minor=(0, 1)))
    product = grad_attn_matmul(cot_pieces, weight_t).reshape(tensor_count, piece_rows, -1)
    order = tensor_pos ^ jnp.arange(tensor_count, dtype=jnp.int32)
    grad_attn = jnp.take(product, order, axis=0).reshape(block_rows, head_count, head_size)

    offsets = jnp.arange(block_rows, dtype=jnp.int32)
    block_order = block_position[0]
    slot_blocks = jnp.take(block_order, context_pos ^ jnp.arange(context_count, dtype=jnp.int32))
    query_positions = slot_blocks[0] * block_rows + offsets
    key_positions = (slot_blocks[:, None] * block_rows + offsets[None, :]).reshape(-1)
    visible = key_positions[None, :] <= query_positions[:, None]

    query_unit, query_inverse = normalize(
        q_pre[0, 0].reshape(block_rows, head_count, head_size).astype(jnp.float32)
    )
    query_norm = (query_unit * q_gain).astype(jnp.bfloat16)
    kv_all = jnp.concatenate(kv_slots, axis=0)
    key_unit, key_inverse = normalize(kv_all[:, :head_size].astype(jnp.float32))
    key_norm = (key_unit * k_gain).astype(jnp.bfloat16)
    value_rows = kv_all[:, head_size:]

    scores = (
        jnp.einsum("qhd,kd->hqk", query_norm, key_norm, preferred_element_type=jnp.float32)
        * score_scale
    )
    scores = jnp.where(visible[None], scores, -jnp.inf)
    row_max = jnp.max(scores, axis=-1, keepdims=True)
    exponent = jnp.exp(scores - row_max)
    probs = exponent / jnp.sum(exponent, axis=-1, keepdims=True)
    grad_prob = jnp.einsum("qhd,kd->hqk", grad_attn, value_rows, preferred_element_type=jnp.float32)
    row_delta = jnp.sum(probs * grad_prob, axis=-1, keepdims=True)
    grad_score = (probs * (grad_prob - row_delta) * score_scale).astype(jnp.bfloat16)
    prob_low = probs.astype(jnp.bfloat16)
    grad_qn = jnp.einsum("hqk,kd->qhd", grad_score, key_norm, preferred_element_type=jnp.float32)
    key_part = jnp.einsum("hqk,qhd->kd", grad_score, query_norm, preferred_element_type=jnp.float32)
    value_part = jnp.einsum("hqk,qhd->kd", prob_low, grad_attn, preferred_element_type=jnp.float32)

    d_query = norm_backward(grad_qn, query_unit, query_inverse, q_gain).astype(jnp.bfloat16)
    gain_query_part = jnp.sum(grad_qn * query_unit, axis=(0, 1))
    gain_key_part = jnp.sum(key_part * key_unit, axis=0)

    gains = jnp.stack([gain_query_part, gain_key_part], axis=0)
    gains = all_sum(gains)

    key_slots = key_part.reshape(context_count, block_rows, head_size)
    value_slots = value_part.reshape(context_count, block_rows, head_size)
    half_index = tensor_pos % per_kv
    key_total = key_slots[0]
    value_total = lax.dynamic_slice_in_dim(value_slots[0], half_index * half_size, half_size, 1)
    group_size = tensor_count * context_count
    for m in range(per_kv):
        for k in range(context_count):
            if m == 0 and k == 0:
                continue
            target_half = (tensor_pos ^ m) % per_kv
            term = jnp.concatenate(
                [
                    key_slots[k],
                    lax.dynamic_slice_in_dim(value_slots[k], target_half * half_size, half_size, 1),
                ],
                axis=1,
            )
            pairs = []
            for source in range(group_size):
                st, sc = divmod(source, context_count)
                pairs.append((source, (st ^ m) * context_count + (sc ^ k)))
            arrived = lax.ppermute(term, ("tensor", "context"), pairs)
            key_total = key_total + arrived[:, :head_size]
            value_total = value_total + arrived[:, head_size:]

    own_unit = key_unit[:block_rows]
    own_inverse = key_inverse[:block_rows]
    d_key_full = norm_backward(key_total, own_unit, own_inverse, k_gain)
    d_key_half = lax.dynamic_slice_in_dim(d_key_full, half_index * half_size, half_size, 1)
    d_key_out = with_layout_constraint(
        d_key_half.astype(jnp.bfloat16).reshape(1, 1, block_rows, half_size), OUT_LAYOUT
    )
    d_value_out = with_layout_constraint(
        value_total.astype(jnp.bfloat16).reshape(1, 1, block_rows, half_size), OUT_LAYOUT
    )
    return (
        d_query.reshape(1, 1, block_rows, head_count * head_size),
        d_key_out,
        d_value_out,
        gains[0],
        gains[1],
    )


def solution(mesh):
    placed = (
        P("dp", "context", None, "tensor"),
        P("dp", "context", None, None),
        P("dp", "context", None, None),
        P("dp", "context", "tensor", None),
        P("tensor", None),
        P(),
        P(),
        P("dp", None),
    )
    return jax.shard_map(
        shard_body,
        mesh=mesh,
        in_specs=placed,
        out_specs=(
            P("dp", "context", None, "tensor"),
            P("dp", "context", None, "tensor"),
            P("dp", "context", None, "tensor"),
            P(),
            P(),
        ),
        check_vma=False,
    )
```

```python
import math

import jax
import jax.numpy as jnp
from jax import lax
from jax.sharding import PartitionSpec as P
from jax.experimental.layout import Layout, with_layout_constraint

EPS = 1e-06
MESH_AXES = ("tensor", "context", "dp")
OUT_LAYOUT = Layout(major_to_minor=(0, 1, 3, 2))


def xor_permute(value, axis, mask):
    size = lax.axis_size(axis)
    return lax.ppermute(value, axis, [(source, source ^ mask) for source in range(size)])


def all_sum(value):
    count = math.prod(lax.axis_size(axis) for axis in MESH_AXES)
    spread = jnp.broadcast_to(value[None], (count,) + value.shape)
    pieces = lax.all_to_all(spread, MESH_AXES, 0, 0, tiled=True)
    total = pieces[0]
    for index in range(1, count):
        total = total + pieces[index]
    return total


def normalize(rows_in):
    inverse = lax.rsqrt(jnp.mean(rows_in * rows_in, axis=-1, keepdims=True) + EPS)
    return (rows_in * inverse, inverse)


def norm_backward(grad_norm, unit_rows, inverse, gain):
    scaled = grad_norm * gain
    return inverse * (scaled - unit_rows * jnp.mean(scaled * unit_rows, axis=-1, keepdims=True))


def shard_body(q_pre, k_pre, values, cotangent, out_weight, q_gain, k_gain, block_position):
    tensor_count = lax.axis_size("tensor")
    context_count = lax.axis_size("context")
    dp_count = lax.axis_size("dp")
    for size in (tensor_count, context_count, dp_count):
        assert size & (size - 1) == 0
    tensor_pos = lax.axis_index("tensor")
    context_pos = lax.axis_index("context")
    head_size = q_gain.shape[0]
    block_rows = q_pre.shape[2]
    head_count = q_pre.shape[3] // head_size
    kv_count = k_pre.shape[3] // head_size
    per_kv = tensor_count // kv_count
    half_size = head_size // per_kv
    kv_column = tensor_pos // per_kv * head_size
    score_scale = 1.0 / math.sqrt(head_size)

    own_kv = jnp.concatenate(
        [
            lax.dynamic_slice_in_dim(k_pre[0, 0], kv_column, head_size, 1),
            lax.dynamic_slice_in_dim(values[0, 0], kv_column, head_size, 1),
        ],
        axis=1,
    )
    kv_slots = [own_kv] + [xor_permute(own_kv, "context", k) for k in range(1, context_count)]

    cot_own = cotangent[0, 0]
    cot_pieces = [cot_own] + [xor_permute(cot_own, "tensor", m) for m in range(1, tensor_count)]
    weight_t = with_layout_constraint(jnp.transpose(out_weight), Layout(major_to_minor=(0, 1)))
    product = lax.dot_general(
        jnp.stack(cot_pieces, axis=0),
        weight_t,
        (((2,), (0,)), ((), ())),
        preferred_element_type=jnp.float32,
    ).astype(jnp.bfloat16)
    order = tensor_pos ^ jnp.arange(tensor_count, dtype=jnp.int32)
    grad_attn = jnp.take(product, order, axis=0).reshape(block_rows, head_count, head_size)

    offsets = jnp.arange(block_rows, dtype=jnp.int32)
    block_order = block_position[0]
    slot_blocks = jnp.take(block_order, context_pos ^ jnp.arange(context_count, dtype=jnp.int32))
    query_positions = slot_blocks[0] * block_rows + offsets
    key_positions = (slot_blocks[:, None] * block_rows + offsets[None, :]).reshape(-1)
    visible = key_positions[None, :] <= query_positions[:, None]

    query_unit, query_inverse = normalize(
        q_pre[0, 0].reshape(block_rows, head_count, head_size).astype(jnp.float32)
    )
    query_norm = (query_unit * q_gain).astype(jnp.bfloat16)
    kv_all = jnp.concatenate(kv_slots, axis=0)
    key_unit, key_inverse = normalize(kv_all[:, :head_size].astype(jnp.float32))
    key_norm = (key_unit * k_gain).astype(jnp.bfloat16)
    value_rows = kv_all[:, head_size:]

    scores = (
        jnp.einsum("qhd,kd->hqk", query_norm, key_norm, preferred_element_type=jnp.float32)
        * score_scale
    )
    scores = jnp.where(visible[None], scores, -jnp.inf)
    row_max = jnp.max(scores, axis=-1, keepdims=True)
    exponent = jnp.exp(scores - row_max)
    probs = exponent / jnp.sum(exponent, axis=-1, keepdims=True)
    grad_prob = jnp.einsum("qhd,kd->hqk", grad_attn, value_rows, preferred_element_type=jnp.float32)
    row_delta = jnp.sum(probs * grad_prob, axis=-1, keepdims=True)
    grad_score = (probs * (grad_prob - row_delta) * score_scale).astype(jnp.bfloat16)
    prob_low = probs.astype(jnp.bfloat16)
    grad_qn = jnp.einsum("hqk,kd->qhd", grad_score, key_norm, preferred_element_type=jnp.float32)
    key_part = jnp.einsum("hqk,qhd->kd", grad_score, query_norm, preferred_element_type=jnp.float32)
    value_part = jnp.einsum("hqk,qhd->kd", prob_low, grad_attn, preferred_element_type=jnp.float32)

    d_query = norm_backward(grad_qn, query_unit, query_inverse, q_gain).astype(jnp.bfloat16)
    gain_query_part = jnp.sum(grad_qn * query_unit, axis=(0, 1))
    gain_key_part = jnp.sum(key_part * key_unit, axis=0)

    gains = jnp.stack([gain_query_part, gain_key_part], axis=0)
    gains = all_sum(gains)

    key_slots = key_part.reshape(context_count, block_rows, head_size)
    value_slots = value_part.reshape(context_count, block_rows, head_size)
    half_index = tensor_pos % per_kv
    key_total = key_slots[0]
    value_total = lax.dynamic_slice_in_dim(value_slots[0], half_index * half_size, half_size, 1)
    group_size = tensor_count * context_count
    for m in range(per_kv):
        for k in range(context_count):
            if m == 0 and k == 0:
                continue
            target_half = (tensor_pos ^ m) % per_kv
            term = jnp.concatenate(
                [
                    key_slots[k],
                    lax.dynamic_slice_in_dim(value_slots[k], target_half * half_size, half_size, 1),
                ],
                axis=1,
            )
            pairs = []
            for source in range(group_size):
                st, sc = divmod(source, context_count)
                pairs.append((source, (st ^ m) * context_count + (sc ^ k)))
            if m:
                term = term.astype(jnp.bfloat16)
            arrived = lax.ppermute(term, ("tensor", "context"), pairs).astype(jnp.float32)
            key_total = key_total + arrived[:, :head_size]
            value_total = value_total + arrived[:, head_size:]

    own_unit = key_unit[:block_rows]
    own_inverse = key_inverse[:block_rows]
    d_key_full = norm_backward(key_total, own_unit, own_inverse, k_gain)
    d_key_half = lax.dynamic_slice_in_dim(d_key_full, half_index * half_size, half_size, 1)
    d_key_out = with_layout_constraint(
        d_key_half.astype(jnp.bfloat16).reshape(1, 1, block_rows, half_size), OUT_LAYOUT
    )
    d_value_out = with_layout_constraint(
        value_total.astype(jnp.bfloat16).reshape(1, 1, block_rows, half_size), OUT_LAYOUT
    )
    return (
        d_query.reshape(1, 1, block_rows, head_count * head_size),
        d_key_out,
        d_value_out,
        gains[0],
        gains[1],
    )


def solution(mesh):
    placed = (
        P("dp", "context", None, "tensor"),
        P("dp", "context", None, None),
        P("dp", "context", None, None),
        P("dp", "context", "tensor", None),
        P("tensor", None),
        P(),
        P(),
        P("dp", None),
    )
    return jax.shard_map(
        shard_body,
        mesh=mesh,
        in_specs=placed,
        out_specs=(
            P("dp", "context", None, "tensor"),
            P("dp", "context", None, "tensor"),
            P("dp", "context", None, "tensor"),
            P(),
            P(),
        ),
        check_vma=False,
    )
```

```python
import math

import jax
import jax.numpy as jnp
from jax import lax
from jax.sharding import PartitionSpec as P
from jax.experimental.layout import Layout, with_layout_constraint

EPS = 1e-06
MESH_AXES = ("tensor", "context", "dp")
OUT_LAYOUT = Layout(major_to_minor=(0, 1, 3, 2))


def xor_permute(value, axis, mask):
    size = lax.axis_size(axis)
    return lax.ppermute(value, axis, [(source, source ^ mask) for source in range(size)])


def all_sum(value):
    count = math.prod(lax.axis_size(axis) for axis in MESH_AXES)
    spread = jnp.broadcast_to(value[None], (count,) + value.shape)
    pieces = lax.all_to_all(spread, MESH_AXES, 0, 0, tiled=True)
    total = pieces[0]
    for index in range(1, count):
        total = total + pieces[index]
    return total


def normalize(rows_in):
    inverse = lax.rsqrt(jnp.mean(rows_in * rows_in, axis=-1, keepdims=True) + EPS)
    return (rows_in * inverse, inverse)


def norm_backward(grad_norm, unit_rows, inverse, gain):
    scaled = grad_norm * gain
    return inverse * (scaled - unit_rows * jnp.mean(scaled * unit_rows, axis=-1, keepdims=True))


def shard_body(q_pre, k_pre, values, cotangent, out_weight, q_gain, k_gain, block_position):
    tensor_count = lax.axis_size("tensor")
    context_count = lax.axis_size("context")
    dp_count = lax.axis_size("dp")
    for size in (tensor_count, context_count, dp_count):
        assert size & (size - 1) == 0
    tensor_pos = lax.axis_index("tensor")
    context_pos = lax.axis_index("context")
    head_size = q_gain.shape[0]
    block_rows = q_pre.shape[2]
    head_count = q_pre.shape[3] // head_size
    kv_count = k_pre.shape[3] // head_size
    per_kv = tensor_count // kv_count
    half_size = head_size // per_kv
    kv_column = tensor_pos // per_kv * head_size
    score_scale = 1.0 / math.sqrt(head_size)

    own_kv = jnp.concatenate(
        [
            lax.dynamic_slice_in_dim(k_pre[0, 0], kv_column, head_size, 1),
            lax.dynamic_slice_in_dim(values[0, 0], kv_column, head_size, 1),
        ],
        axis=1,
    )
    kv_slots = [own_kv] + [xor_permute(own_kv, "context", k) for k in range(1, context_count)]

    cot_own = cotangent[0, 0]
    cot_pieces = [cot_own] + [xor_permute(cot_own, "tensor", m) for m in range(1, tensor_count)]
    piece_rows = cot_own.shape[0]
    weight_t = with_layout_constraint(jnp.transpose(out_weight), Layout(major_to_minor=(0, 1)))
    product = lax.dot_general(
        jnp.stack(cot_pieces, axis=0),
        weight_t,
        (((2,), (0,)), ((), ())),
        preferred_element_type=jnp.float32,
    ).astype(jnp.bfloat16)
    order = tensor_pos ^ jnp.arange(tensor_count, dtype=jnp.int32)
    grad_attn = product.reshape(block_rows, head_count, head_size)

    offsets = jnp.arange(block_rows, dtype=jnp.int32)
    block_order = block_position[0]
    slot_blocks = jnp.take(block_order, context_pos ^ jnp.arange(context_count, dtype=jnp.int32))
    query_positions = (
        slot_blocks[0] * block_rows + order[:, None] * piece_rows + offsets[None, :piece_rows]
    ).reshape(-1)
    key_positions = (slot_blocks[:, None] * block_rows + offsets[None, :]).reshape(-1)
    visible = key_positions[None, :] <= query_positions[:, None]

    query_rows = q_pre[0, 0].reshape(tensor_count, piece_rows, head_count, head_size)
    query_rows = jnp.take(query_rows, order, axis=0).reshape(block_rows, head_count, head_size)
    query_unit, query_inverse = normalize(query_rows.astype(jnp.float32))
    query_norm = (query_unit * q_gain).astype(jnp.bfloat16)
    kv_all = jnp.concatenate(kv_slots, axis=0)
    key_unit, key_inverse = normalize(kv_all[:, :head_size].astype(jnp.float32))
    key_norm = (key_unit * k_gain).astype(jnp.bfloat16)
    value_rows = kv_all[:, head_size:]

    scores = (
        jnp.einsum("qhd,kd->hqk", query_norm, key_norm, preferred_element_type=jnp.float32)
        * score_scale
    )
    scores = jnp.where(visible[None], scores, -jnp.inf)
    row_max = jnp.max(scores, axis=-1, keepdims=True)
    exponent = jnp.exp(scores - row_max)
    probs = exponent / jnp.sum(exponent, axis=-1, keepdims=True)
    grad_prob = jnp.einsum("qhd,kd->hqk", grad_attn, value_rows, preferred_element_type=jnp.float32)
    row_delta = jnp.sum(probs * grad_prob, axis=-1, keepdims=True)
    grad_score = (probs * (grad_prob - row_delta) * score_scale).astype(jnp.bfloat16)
    prob_low = probs.astype(jnp.bfloat16)
    grad_qn = jnp.einsum("hqk,kd->qhd", grad_score, key_norm, preferred_element_type=jnp.float32)
    key_part = jnp.einsum("hqk,qhd->kd", grad_score, query_norm, preferred_element_type=jnp.float32)
    value_part = jnp.einsum("hqk,qhd->kd", prob_low, grad_attn, preferred_element_type=jnp.float32)

    d_query = norm_backward(grad_qn, query_unit, query_inverse, q_gain).astype(jnp.bfloat16)
    d_query = jnp.take(d_query.reshape(tensor_count, piece_rows, -1), order, axis=0)
    gain_query_part = jnp.sum(grad_qn * query_unit, axis=(0, 1))
    gain_key_part = jnp.sum(key_part * key_unit, axis=0)

    gains = jnp.stack([gain_query_part, gain_key_part], axis=0)
    gains = all_sum(gains)

    key_slots = key_part.reshape(context_count, block_rows, head_size)
    value_slots = value_part.reshape(context_count, block_rows, head_size)
    half_index = tensor_pos % per_kv
    key_total = key_slots[0]
    value_total = lax.dynamic_slice_in_dim(value_slots[0], half_index * half_size, half_size, 1)
    group_size = tensor_count * context_count
    for m in range(per_kv):
        for k in range(context_count):
            if m == 0 and k == 0:
                continue
            target_half = (tensor_pos ^ m) % per_kv
            term = jnp.concatenate(
                [
                    key_slots[k],
                    lax.dynamic_slice_in_dim(value_slots[k], target_half * half_size, half_size, 1),
                ],
                axis=1,
            )
            pairs = []
            for source in range(group_size):
                st, sc = divmod(source, context_count)
                pairs.append((source, (st ^ m) * context_count + (sc ^ k)))
            if m:
                term = term.astype(jnp.bfloat16)
            arrived = lax.ppermute(term, ("tensor", "context"), pairs).astype(jnp.float32)
            key_total = key_total + arrived[:, :head_size]
            value_total = value_total + arrived[:, head_size:]

    own_unit = key_unit[:block_rows]
    own_inverse = key_inverse[:block_rows]
    d_key_full = norm_backward(key_total, own_unit, own_inverse, k_gain)
    d_key_half = lax.dynamic_slice_in_dim(d_key_full, half_index * half_size, half_size, 1)
    d_key_out = with_layout_constraint(
        d_key_half.astype(jnp.bfloat16).reshape(1, 1, block_rows, half_size), OUT_LAYOUT
    )
    d_value_out = with_layout_constraint(
        value_total.astype(jnp.bfloat16).reshape(1, 1, block_rows, half_size), OUT_LAYOUT
    )
    return (
        d_query.reshape(1, 1, block_rows, head_count * head_size),
        d_key_out,
        d_value_out,
        gains[0],
        gains[1],
    )


def solution(mesh):
    placed = (
        P("dp", "context", None, "tensor"),
        P("dp", "context", None, None),
        P("dp", "context", None, None),
        P("dp", "context", "tensor", None),
        P("tensor", None),
        P(),
        P(),
        P("dp", None),
    )
    return jax.shard_map(
        shard_body,
        mesh=mesh,
        in_specs=placed,
        out_specs=(
            P("dp", "context", None, "tensor"),
            P("dp", "context", None, "tensor"),
            P("dp", "context", None, "tensor"),
            P(),
            P(),
        ),
        check_vma=False,
    )
```

```python
import math

import jax
import jax.numpy as jnp
from jax import lax
from jax.sharding import PartitionSpec as P
from jax.experimental.layout import Layout, with_layout_constraint

EPS = 1e-06
MESH_AXES = ("tensor", "context", "dp")
OUT_LAYOUT = Layout(major_to_minor=(0, 1, 3, 2))


def xor_permute(value, axis, mask):
    size = lax.axis_size(axis)
    return lax.ppermute(value, axis, [(source, source ^ mask) for source in range(size)])


def all_sum(value):
    count = math.prod(lax.axis_size(axis) for axis in MESH_AXES)
    spread = jnp.broadcast_to(value[None], (count,) + value.shape)
    pieces = lax.all_to_all(spread, MESH_AXES, 0, 0, tiled=True)
    total = pieces[0]
    for index in range(1, count):
        total = total + pieces[index]
    return total


def normalize(rows_in):
    inverse = lax.rsqrt(jnp.mean(rows_in * rows_in, axis=-1, keepdims=True) + EPS)
    return (rows_in * inverse, inverse)


def norm_backward(grad_norm, unit_rows, inverse, gain):
    scaled = grad_norm * gain
    return inverse * (scaled - unit_rows * jnp.mean(scaled * unit_rows, axis=-1, keepdims=True))


def shard_body(q_pre, k_pre, values, cotangent, out_weight, q_gain, k_gain, block_position):
    tensor_count = lax.axis_size("tensor")
    context_count = lax.axis_size("context")
    dp_count = lax.axis_size("dp")
    for size in (tensor_count, context_count, dp_count):
        assert size & (size - 1) == 0
    tensor_pos = lax.axis_index("tensor")
    context_pos = lax.axis_index("context")
    head_size = q_gain.shape[0]
    block_rows = q_pre.shape[2]
    head_count = q_pre.shape[3] // head_size
    kv_count = k_pre.shape[3] // head_size
    per_kv = tensor_count // kv_count
    half_size = head_size // per_kv
    kv_column = tensor_pos // per_kv * head_size
    score_scale = 1.0 / math.sqrt(head_size)

    own_kv = jnp.concatenate(
        [
            lax.dynamic_slice_in_dim(k_pre[0, 0], kv_column, head_size, 1),
            lax.dynamic_slice_in_dim(values[0, 0], kv_column, head_size, 1),
        ],
        axis=1,
    )
    kv_slots = [own_kv] + [xor_permute(own_kv, "context", k) for k in range(1, context_count)]

    cot_own = cotangent[0, 0]
    _, features = cot_own.shape
    split = features // 2
    weight_t = with_layout_constraint(jnp.transpose(out_weight), Layout(major_to_minor=(0, 1)))
    product = None
    for lo, hi in ((0, split), (split, features)):
        cot_half = cot_own[:, lo:hi]
        pieces = [cot_half] + [xor_permute(cot_half, "tensor", m) for m in range(1, tensor_count)]
        partial = lax.dot_general(
            jnp.stack(pieces, axis=0),
            weight_t[lo:hi],
            (((2,), (0,)), ((), ())),
            preferred_element_type=jnp.float32,
        )
        if product is None:
            product = lax.optimization_barrier(partial)
        else:
            product = product + partial
    product = product.astype(jnp.bfloat16)
    order = tensor_pos ^ jnp.arange(tensor_count, dtype=jnp.int32)
    grad_attn = jnp.take(product, order, axis=0).reshape(block_rows, head_count, head_size)

    offsets = jnp.arange(block_rows, dtype=jnp.int32)
    block_order = block_position[0]
    slot_blocks = jnp.take(block_order, context_pos ^ jnp.arange(context_count, dtype=jnp.int32))
    query_positions = slot_blocks[0] * block_rows + offsets
    key_positions = (slot_blocks[:, None] * block_rows + offsets[None, :]).reshape(-1)
    visible = key_positions[None, :] <= query_positions[:, None]

    query_unit, query_inverse = normalize(
        q_pre[0, 0].reshape(block_rows, head_count, head_size).astype(jnp.float32)
    )
    query_norm = (query_unit * q_gain).astype(jnp.bfloat16)
    kv_all = jnp.concatenate(kv_slots, axis=0)
    key_unit, key_inverse = normalize(kv_all[:, :head_size].astype(jnp.float32))
    key_norm = (key_unit * k_gain).astype(jnp.bfloat16)
    value_rows = kv_all[:, head_size:]

    scores = (
        jnp.einsum("qhd,kd->hqk", query_norm, key_norm, preferred_element_type=jnp.float32)
        * score_scale
    )
    scores = jnp.where(visible[None], scores, -jnp.inf)
    row_max = jnp.max(scores, axis=-1, keepdims=True)
    exponent = jnp.exp(scores - row_max)
    probs = exponent / jnp.sum(exponent, axis=-1, keepdims=True)
    grad_prob = jnp.einsum("qhd,kd->hqk", grad_attn, value_rows, preferred_element_type=jnp.float32)
    row_delta = jnp.sum(probs * grad_prob, axis=-1, keepdims=True)
    grad_score = (probs * (grad_prob - row_delta) * score_scale).astype(jnp.bfloat16)
    prob_low = probs.astype(jnp.bfloat16)
    grad_qn = jnp.einsum("hqk,kd->qhd", grad_score, key_norm, preferred_element_type=jnp.float32)
    key_part = jnp.einsum("hqk,qhd->kd", grad_score, query_norm, preferred_element_type=jnp.float32)
    value_part = jnp.einsum("hqk,qhd->kd", prob_low, grad_attn, preferred_element_type=jnp.float32)

    d_query = norm_backward(grad_qn, query_unit, query_inverse, q_gain).astype(jnp.bfloat16)
    gain_query_part = jnp.sum(grad_qn * query_unit, axis=(0, 1))
    gain_key_part = jnp.sum(key_part * key_unit, axis=0)

    gains = jnp.stack([gain_query_part, gain_key_part], axis=0)
    gains = all_sum(gains)

    key_slots = key_part.reshape(context_count, block_rows, head_size)
    value_slots = value_part.reshape(context_count, block_rows, head_size)
    half_index = tensor_pos % per_kv
    key_total = key_slots[0]
    value_total = lax.dynamic_slice_in_dim(value_slots[0], half_index * half_size, half_size, 1)
    group_size = tensor_count * context_count
    for m in range(per_kv):
        for k in range(context_count):
            if m == 0 and k == 0:
                continue
            target_half = (tensor_pos ^ m) % per_kv
            term = jnp.concatenate(
                [
                    key_slots[k],
                    lax.dynamic_slice_in_dim(value_slots[k], target_half * half_size, half_size, 1),
                ],
                axis=1,
            )
            pairs = []
            for source in range(group_size):
                st, sc = divmod(source, context_count)
                pairs.append((source, (st ^ m) * context_count + (sc ^ k)))
            if m:
                term = term.astype(jnp.bfloat16)
            arrived = lax.ppermute(term, ("tensor", "context"), pairs).astype(jnp.float32)
            key_total = key_total + arrived[:, :head_size]
            value_total = value_total + arrived[:, head_size:]

    own_unit = key_unit[:block_rows]
    own_inverse = key_inverse[:block_rows]
    d_key_full = norm_backward(key_total, own_unit, own_inverse, k_gain)
    d_key_half = lax.dynamic_slice_in_dim(d_key_full, half_index * half_size, half_size, 1)
    d_key_out = with_layout_constraint(
        d_key_half.astype(jnp.bfloat16).reshape(1, 1, block_rows, half_size), OUT_LAYOUT
    )
    d_value_out = with_layout_constraint(
        value_total.astype(jnp.bfloat16).reshape(1, 1, block_rows, half_size), OUT_LAYOUT
    )
    return (
        d_query.reshape(1, 1, block_rows, head_count * head_size),
        d_key_out,
        d_value_out,
        gains[0],
        gains[1],
    )


def solution(mesh):
    placed = (
        P("dp", "context", None, "tensor"),
        P("dp", "context", None, None),
        P("dp", "context", None, None),
        P("dp", "context", "tensor", None),
        P("tensor", None),
        P(),
        P(),
        P("dp", None),
    )
    return jax.shard_map(
        shard_body,
        mesh=mesh,
        in_specs=placed,
        out_specs=(
            P("dp", "context", None, "tensor"),
            P("dp", "context", None, "tensor"),
            P("dp", "context", None, "tensor"),
            P(),
            P(),
        ),
        check_vma=False,
    )
```

```python
import math

import jax
import jax.numpy as jnp
from jax import lax
from jax.sharding import PartitionSpec as P
from jax.experimental.layout import Layout, with_layout_constraint

EPS = 1e-06
MESH_AXES = ("tensor", "context", "dp")
OUT_LAYOUT = Layout(major_to_minor=(0, 1, 3, 2))


def xor_permute(value, axis, mask):
    size = lax.axis_size(axis)
    return lax.ppermute(value, axis, [(source, source ^ mask) for source in range(size)])


def all_sum(value):
    count = math.prod(lax.axis_size(axis) for axis in MESH_AXES)
    spread = jnp.broadcast_to(value[None], (count,) + value.shape)
    pieces = lax.all_to_all(spread, MESH_AXES, 0, 0, tiled=True)
    total = pieces[0]
    for index in range(1, count):
        total = total + pieces[index]
    return total


def normalize(rows_in):
    inverse = lax.rsqrt(jnp.mean(rows_in * rows_in, axis=-1, keepdims=True) + EPS)
    return (rows_in * inverse, inverse)


def norm_backward(grad_norm, unit_rows, inverse, gain):
    scaled = grad_norm * gain
    return inverse * (scaled - unit_rows * jnp.mean(scaled * unit_rows, axis=-1, keepdims=True))


def shard_body(q_pre, k_pre, values, cotangent, out_weight, q_gain, k_gain, block_position):
    tensor_count = lax.axis_size("tensor")
    context_count = lax.axis_size("context")
    dp_count = lax.axis_size("dp")
    for size in (tensor_count, context_count, dp_count):
        assert size & (size - 1) == 0
    tensor_pos = lax.axis_index("tensor")
    context_pos = lax.axis_index("context")
    head_size = q_gain.shape[0]
    block_rows = q_pre.shape[2]
    head_count = q_pre.shape[3] // head_size
    kv_count = k_pre.shape[3] // head_size
    per_kv = tensor_count // kv_count
    half_size = head_size // per_kv
    kv_column = tensor_pos // per_kv * head_size
    score_scale = 1.0 / math.sqrt(head_size)

    own_kv = jnp.concatenate(
        [
            lax.dynamic_slice_in_dim(k_pre[0, 0], kv_column, head_size, 1),
            lax.dynamic_slice_in_dim(values[0, 0], kv_column, head_size, 1),
        ],
        axis=1,
    )
    kv_slots = [own_kv] + [xor_permute(own_kv, "context", k) for k in range(1, context_count)]

    cot_own = cotangent[0, 0]
    cot_pieces = [cot_own] + [xor_permute(cot_own, "tensor", m) for m in range(1, tensor_count)]
    weight_t = with_layout_constraint(jnp.transpose(out_weight), Layout(major_to_minor=(0, 1)))
    stacked = jnp.stack(cot_pieces, axis=0)
    features = stacked.shape[2]
    split = features // 2
    product = None
    for lo, hi in ((0, split), (split, features)):
        partial = lax.dot_general(
            stacked[:, :, lo:hi],
            weight_t[lo:hi],
            (((2,), (0,)), ((), ())),
            preferred_element_type=jnp.float32,
        )
        product = lax.optimization_barrier(partial) if product is None else product + partial
    product = product.astype(jnp.bfloat16)
    order = tensor_pos ^ jnp.arange(tensor_count, dtype=jnp.int32)
    grad_attn = jnp.take(product, order, axis=0).reshape(block_rows, head_count, head_size)

    offsets = jnp.arange(block_rows, dtype=jnp.int32)
    block_order = block_position[0]
    slot_blocks = jnp.take(block_order, context_pos ^ jnp.arange(context_count, dtype=jnp.int32))
    query_positions = slot_blocks[0] * block_rows + offsets
    key_positions = (slot_blocks[:, None] * block_rows + offsets[None, :]).reshape(-1)
    visible = key_positions[None, :] <= query_positions[:, None]

    query_unit, query_inverse = normalize(
        q_pre[0, 0].reshape(block_rows, head_count, head_size).astype(jnp.float32)
    )
    query_norm = (query_unit * q_gain).astype(jnp.bfloat16)
    kv_all = jnp.concatenate(kv_slots, axis=0)
    key_unit, key_inverse = normalize(kv_all[:, :head_size].astype(jnp.float32))
    key_norm = (key_unit * k_gain).astype(jnp.bfloat16)
    value_rows = kv_all[:, head_size:]

    scores = (
        jnp.einsum("qhd,kd->hqk", query_norm, key_norm, preferred_element_type=jnp.float32)
        * score_scale
    )
    scores = jnp.where(visible[None], scores, -jnp.inf)
    row_max = jnp.max(scores, axis=-1, keepdims=True)
    exponent = jnp.exp(scores - row_max)
    probs = exponent / jnp.sum(exponent, axis=-1, keepdims=True)
    grad_prob = jnp.einsum("qhd,kd->hqk", grad_attn, value_rows, preferred_element_type=jnp.float32)
    row_delta = jnp.sum(probs * grad_prob, axis=-1, keepdims=True)
    grad_score = (probs * (grad_prob - row_delta) * score_scale).astype(jnp.bfloat16)
    prob_low = probs.astype(jnp.bfloat16)
    grad_qn = jnp.einsum("hqk,kd->qhd", grad_score, key_norm, preferred_element_type=jnp.float32)
    key_part = jnp.einsum("hqk,qhd->kd", grad_score, query_norm, preferred_element_type=jnp.float32)
    value_part = jnp.einsum("hqk,qhd->kd", prob_low, grad_attn, preferred_element_type=jnp.float32)

    d_query = norm_backward(grad_qn, query_unit, query_inverse, q_gain).astype(jnp.bfloat16)
    gain_query_part = jnp.sum(grad_qn * query_unit, axis=(0, 1))
    gain_key_part = jnp.sum(key_part * key_unit, axis=0)

    gains = jnp.stack([gain_query_part, gain_key_part], axis=0)
    gains = all_sum(gains)

    key_slots = key_part.reshape(context_count, block_rows, head_size)
    value_slots = value_part.reshape(context_count, block_rows, head_size)
    half_index = tensor_pos % per_kv
    key_total = key_slots[0]
    value_total = lax.dynamic_slice_in_dim(value_slots[0], half_index * half_size, half_size, 1)
    group_size = tensor_count * context_count
    for m in range(per_kv):
        for k in range(context_count):
            if m == 0 and k == 0:
                continue
            target_half = (tensor_pos ^ m) % per_kv
            term = jnp.concatenate(
                [
                    key_slots[k],
                    lax.dynamic_slice_in_dim(value_slots[k], target_half * half_size, half_size, 1),
                ],
                axis=1,
            )
            pairs = []
            for source in range(group_size):
                st, sc = divmod(source, context_count)
                pairs.append((source, (st ^ m) * context_count + (sc ^ k)))
            if m:
                term = term.astype(jnp.bfloat16)
            arrived = lax.ppermute(term, ("tensor", "context"), pairs).astype(jnp.float32)
            key_total = key_total + arrived[:, :head_size]
            value_total = value_total + arrived[:, head_size:]

    own_unit = key_unit[:block_rows]
    own_inverse = key_inverse[:block_rows]
    d_key_full = norm_backward(key_total, own_unit, own_inverse, k_gain)
    d_key_half = lax.dynamic_slice_in_dim(d_key_full, half_index * half_size, half_size, 1)
    d_key_out = with_layout_constraint(
        d_key_half.astype(jnp.bfloat16).reshape(1, 1, block_rows, half_size), OUT_LAYOUT
    )
    d_value_out = with_layout_constraint(
        value_total.astype(jnp.bfloat16).reshape(1, 1, block_rows, half_size), OUT_LAYOUT
    )
    return (
        d_query.reshape(1, 1, block_rows, head_count * head_size),
        d_key_out,
        d_value_out,
        gains[0],
        gains[1],
    )


def solution(mesh):
    placed = (
        P("dp", "context", None, "tensor"),
        P("dp", "context", None, None),
        P("dp", "context", None, None),
        P("dp", "context", "tensor", None),
        P("tensor", None),
        P(),
        P(),
        P("dp", None),
    )
    return jax.shard_map(
        shard_body,
        mesh=mesh,
        in_specs=placed,
        out_specs=(
            P("dp", "context", None, "tensor"),
            P("dp", "context", None, "tensor"),
            P("dp", "context", None, "tensor"),
            P(),
            P(),
        ),
        check_vma=False,
    )
```

```python
import math

import jax
import jax.numpy as jnp
from jax import lax
from jax.sharding import PartitionSpec as P
from jax.experimental.layout import Layout, with_layout_constraint

EPS = 1e-06
MESH_AXES = ("tensor", "context", "dp")
OUT_LAYOUT = Layout(major_to_minor=(0, 1, 3, 2))


def xor_permute(value, axis, mask):
    size = lax.axis_size(axis)
    return lax.ppermute(value, axis, [(source, source ^ mask) for source in range(size)])


def all_sum(value):
    count = math.prod(lax.axis_size(axis) for axis in MESH_AXES)
    spread = jnp.broadcast_to(value[None], (count,) + value.shape)
    pieces = lax.all_to_all(spread, MESH_AXES, 0, 0, tiled=True)
    total = pieces[0]
    for index in range(1, count):
        total = total + pieces[index]
    return total


def normalize(rows_in):
    inverse = lax.rsqrt(jnp.mean(rows_in * rows_in, axis=-1, keepdims=True) + EPS)
    return (rows_in * inverse, inverse)


def norm_backward(grad_norm, unit_rows, inverse, gain):
    scaled = grad_norm * gain
    return inverse * (scaled - unit_rows * jnp.mean(scaled * unit_rows, axis=-1, keepdims=True))


def shard_body(q_pre, k_pre, values, cotangent, out_weight, q_gain, k_gain, block_position):
    tensor_count = lax.axis_size("tensor")
    context_count = lax.axis_size("context")
    dp_count = lax.axis_size("dp")
    for size in (tensor_count, context_count, dp_count):
        assert size & (size - 1) == 0
    tensor_pos = lax.axis_index("tensor")
    context_pos = lax.axis_index("context")
    head_size = q_gain.shape[0]
    block_rows = q_pre.shape[2]
    head_count = q_pre.shape[3] // head_size
    kv_count = k_pre.shape[3] // head_size
    per_kv = tensor_count // kv_count
    half_size = head_size // per_kv
    kv_column = tensor_pos // per_kv * head_size
    score_scale = 1.0 / math.sqrt(head_size)

    own_kv = jnp.concatenate(
        [
            lax.dynamic_slice_in_dim(k_pre[0, 0], kv_column, head_size, 1),
            lax.dynamic_slice_in_dim(values[0, 0], kv_column, head_size, 1),
        ],
        axis=1,
    )
    kv_slots = [own_kv] + [xor_permute(own_kv, "context", k) for k in range(1, context_count)]

    cot_own = cotangent[0, 0]
    cot_pieces = [cot_own] + [xor_permute(cot_own, "tensor", m) for m in range(1, tensor_count)]
    piece_rows = cot_own.shape[0]
    weight_t = with_layout_constraint(jnp.transpose(out_weight), Layout(major_to_minor=(0, 1)))
    stacked = jnp.stack(cot_pieces, axis=0)
    features = stacked.shape[2]
    split = features // 2
    product = None
    for lo, hi in ((0, split), (split, features)):
        partial = lax.dot_general(
            stacked[:, :, lo:hi],
            weight_t[lo:hi],
            (((2,), (0,)), ((), ())),
            preferred_element_type=jnp.float32,
        )
        product = lax.optimization_barrier(partial) if product is None else product + partial
    product = product.astype(jnp.bfloat16)
    order = tensor_pos ^ jnp.arange(tensor_count, dtype=jnp.int32)
    grad_attn = product.reshape(block_rows, head_count, head_size)

    offsets = jnp.arange(block_rows, dtype=jnp.int32)
    block_order = block_position[0]
    slot_blocks = jnp.take(block_order, context_pos ^ jnp.arange(context_count, dtype=jnp.int32))
    query_positions = (
        slot_blocks[0] * block_rows + order[:, None] * piece_rows + offsets[None, :piece_rows]
    ).reshape(-1)
    key_positions = (slot_blocks[:, None] * block_rows + offsets[None, :]).reshape(-1)
    visible = key_positions[None, :] <= query_positions[:, None]

    query_rows = q_pre[0, 0].reshape(tensor_count, piece_rows, head_count, head_size)
    query_rows = jnp.take(query_rows, order, axis=0).reshape(block_rows, head_count, head_size)
    query_unit, query_inverse = normalize(query_rows.astype(jnp.float32))
    query_norm = (query_unit * q_gain).astype(jnp.bfloat16)
    kv_all = jnp.concatenate(kv_slots, axis=0)
    key_unit, key_inverse = normalize(kv_all[:, :head_size].astype(jnp.float32))
    key_norm = (key_unit * k_gain).astype(jnp.bfloat16)
    value_rows = kv_all[:, head_size:]

    scores = (
        jnp.einsum("qhd,kd->hqk", query_norm, key_norm, preferred_element_type=jnp.float32)
        * score_scale
    )
    scores = jnp.where(visible[None], scores, -jnp.inf)
    row_max = jnp.max(scores, axis=-1, keepdims=True)
    exponent = jnp.exp(scores - row_max)
    probs = exponent / jnp.sum(exponent, axis=-1, keepdims=True)
    grad_prob = jnp.einsum("qhd,kd->hqk", grad_attn, value_rows, preferred_element_type=jnp.float32)
    row_delta = jnp.sum(probs * grad_prob, axis=-1, keepdims=True)
    grad_score = (probs * (grad_prob - row_delta) * score_scale).astype(jnp.bfloat16)
    prob_low = probs.astype(jnp.bfloat16)
    grad_qn = jnp.einsum("hqk,kd->qhd", grad_score, key_norm, preferred_element_type=jnp.float32)
    key_part = jnp.einsum("hqk,qhd->kd", grad_score, query_norm, preferred_element_type=jnp.float32)
    value_part = jnp.einsum("hqk,qhd->kd", prob_low, grad_attn, preferred_element_type=jnp.float32)

    d_query = norm_backward(grad_qn, query_unit, query_inverse, q_gain).astype(jnp.bfloat16)
    d_query = jnp.take(d_query.reshape(tensor_count, piece_rows, -1), order, axis=0)
    gain_query_part = jnp.sum(grad_qn * query_unit, axis=(0, 1))
    gain_key_part = jnp.sum(key_part * key_unit, axis=0)

    gains = jnp.stack([gain_query_part, gain_key_part], axis=0)
    gains = all_sum(gains)

    key_slots = key_part.reshape(context_count, block_rows, head_size)
    value_slots = value_part.reshape(context_count, block_rows, head_size)
    half_index = tensor_pos % per_kv
    key_total = key_slots[0]
    value_total = lax.dynamic_slice_in_dim(value_slots[0], half_index * half_size, half_size, 1)
    group_size = tensor_count * context_count
    for m in range(per_kv):
        for k in range(context_count):
            if m == 0 and k == 0:
                continue
            target_half = (tensor_pos ^ m) % per_kv
            term = jnp.concatenate(
                [
                    key_slots[k],
                    lax.dynamic_slice_in_dim(value_slots[k], target_half * half_size, half_size, 1),
                ],
                axis=1,
            )
            pairs = []
            for source in range(group_size):
                st, sc = divmod(source, context_count)
                pairs.append((source, (st ^ m) * context_count + (sc ^ k)))
            if m:
                term = term.astype(jnp.bfloat16)
            arrived = lax.ppermute(term, ("tensor", "context"), pairs).astype(jnp.float32)
            key_total = key_total + arrived[:, :head_size]
            value_total = value_total + arrived[:, head_size:]

    own_unit = key_unit[:block_rows]
    own_inverse = key_inverse[:block_rows]
    d_key_full = norm_backward(key_total, own_unit, own_inverse, k_gain)
    d_key_half = lax.dynamic_slice_in_dim(d_key_full, half_index * half_size, half_size, 1)
    d_key_out = with_layout_constraint(
        d_key_half.astype(jnp.bfloat16).reshape(1, 1, block_rows, half_size), OUT_LAYOUT
    )
    d_value_out = with_layout_constraint(
        value_total.astype(jnp.bfloat16).reshape(1, 1, block_rows, half_size), OUT_LAYOUT
    )
    return (
        d_query.reshape(1, 1, block_rows, head_count * head_size),
        d_key_out,
        d_value_out,
        gains[0],
        gains[1],
    )


def solution(mesh):
    placed = (
        P("dp", "context", None, "tensor"),
        P("dp", "context", None, None),
        P("dp", "context", None, None),
        P("dp", "context", "tensor", None),
        P("tensor", None),
        P(),
        P(),
        P("dp", None),
    )
    return jax.shard_map(
        shard_body,
        mesh=mesh,
        in_specs=placed,
        out_specs=(
            P("dp", "context", None, "tensor"),
            P("dp", "context", None, "tensor"),
            P("dp", "context", None, "tensor"),
            P(),
            P(),
        ),
        check_vma=False,
    )
```

```python
import math

import jax
import jax.numpy as jnp
from jax import lax
from jax.sharding import PartitionSpec as P
from jax.experimental.layout import Layout, with_layout_constraint

EPS = 1e-06
MESH_AXES = ("tensor", "context", "dp")
OUT_LAYOUT = Layout(major_to_minor=(0, 1, 3, 2))


def xor_permute(value, axis, mask):
    size = lax.axis_size(axis)
    return lax.ppermute(value, axis, [(source, source ^ mask) for source in range(size)])


def all_sum(value):
    count = math.prod(lax.axis_size(axis) for axis in MESH_AXES)
    spread = jnp.broadcast_to(value[None], (count,) + value.shape)
    pieces = lax.all_to_all(spread, MESH_AXES, 0, 0, tiled=True)
    return jnp.sum(pieces, axis=0)


def normalize(rows_in):
    inverse = lax.rsqrt(jnp.mean(rows_in * rows_in, axis=-1, keepdims=True) + EPS)
    return (rows_in * inverse, inverse)


def norm_backward(grad_norm, unit_rows, inverse, gain):
    scaled = grad_norm * gain
    return inverse * (scaled - unit_rows * jnp.mean(scaled * unit_rows, axis=-1, keepdims=True))


def shard_body(q_pre, k_pre, values, cotangent, out_weight, q_gain, k_gain, block_position):
    tensor_count = lax.axis_size("tensor")
    context_count = lax.axis_size("context")
    dp_count = lax.axis_size("dp")
    for size in (tensor_count, context_count, dp_count):
        assert size & (size - 1) == 0
    tensor_pos = lax.axis_index("tensor")
    context_pos = lax.axis_index("context")
    head_size = q_gain.shape[0]
    block_rows = q_pre.shape[2]
    head_count = q_pre.shape[3] // head_size
    kv_count = k_pre.shape[3] // head_size
    per_kv = tensor_count // kv_count
    half_size = head_size // per_kv
    kv_column = tensor_pos // per_kv * head_size
    score_scale = 1.0 / math.sqrt(head_size)

    own_kv = jnp.concatenate(
        [
            lax.dynamic_slice_in_dim(k_pre[0, 0], kv_column, head_size, 1),
            lax.dynamic_slice_in_dim(values[0, 0], kv_column, head_size, 1),
        ],
        axis=1,
    )
    kv_slots = [own_kv] + [xor_permute(own_kv, "context", k) for k in range(1, context_count)]

    cot_own = cotangent[0, 0]
    cot_pieces = [cot_own] + [xor_permute(cot_own, "tensor", m) for m in range(1, tensor_count)]
    weight_t = with_layout_constraint(jnp.transpose(out_weight), Layout(major_to_minor=(0, 1)))
    stacked = jnp.stack(cot_pieces, axis=0)
    features = stacked.shape[2]
    split = features // 2
    product = None
    for lo, hi in ((0, split), (split, features)):
        partial = lax.dot_general(
            stacked[:, :, lo:hi],
            weight_t[lo:hi],
            (((2,), (0,)), ((), ())),
            preferred_element_type=jnp.float32,
        )
        product = lax.optimization_barrier(partial) if product is None else product + partial
    product = product.astype(jnp.bfloat16)
    order = tensor_pos ^ jnp.arange(tensor_count, dtype=jnp.int32)
    grad_attn = jnp.take(product, order, axis=0).reshape(block_rows, head_count, head_size)

    offsets = jnp.arange(block_rows, dtype=jnp.int32)
    block_order = block_position[0]
    slot_blocks = jnp.take(block_order, context_pos ^ jnp.arange(context_count, dtype=jnp.int32))
    query_positions = slot_blocks[0] * block_rows + offsets
    key_positions = (slot_blocks[:, None] * block_rows + offsets[None, :]).reshape(-1)
    visible = key_positions[None, :] <= query_positions[:, None]

    query_unit, query_inverse = normalize(
        q_pre[0, 0].reshape(block_rows, head_count, head_size).astype(jnp.float32)
    )
    query_norm = (query_unit * q_gain).astype(jnp.bfloat16)
    kv_all = jnp.concatenate(kv_slots, axis=0)
    key_unit, key_inverse = normalize(kv_all[:, :head_size].astype(jnp.float32))
    key_norm = (key_unit * k_gain).astype(jnp.bfloat16)
    value_rows = kv_all[:, head_size:]

    scores = (
        jnp.einsum("qhd,kd->hqk", query_norm, key_norm, preferred_element_type=jnp.float32)
        * score_scale
    )
    scores = jnp.where(visible[None], scores, -jnp.inf)
    row_max = jnp.max(scores, axis=-1, keepdims=True)
    exponent = jnp.exp(scores - row_max)
    probs = exponent / jnp.sum(exponent, axis=-1, keepdims=True)
    grad_prob = jnp.einsum("qhd,kd->hqk", grad_attn, value_rows, preferred_element_type=jnp.float32)
    row_delta = jnp.sum(probs * grad_prob, axis=-1, keepdims=True)
    grad_score = (probs * (grad_prob - row_delta) * score_scale).astype(jnp.bfloat16)
    prob_low = probs.astype(jnp.bfloat16)
    grad_qn = jnp.einsum("hqk,kd->qhd", grad_score, key_norm, preferred_element_type=jnp.float32)
    key_part = jnp.einsum("hqk,qhd->kd", grad_score, query_norm, preferred_element_type=jnp.float32)
    value_part = jnp.einsum("hqk,qhd->kd", prob_low, grad_attn, preferred_element_type=jnp.float32)

    d_query = norm_backward(grad_qn, query_unit, query_inverse, q_gain).astype(jnp.bfloat16)
    gain_query_part = jnp.sum(grad_qn * query_unit, axis=(0, 1))
    gain_key_part = jnp.sum(key_part * key_unit, axis=0)

    gains = jnp.stack([gain_query_part, gain_key_part], axis=0)
    gains = all_sum(gains)

    key_slots = key_part.reshape(context_count, block_rows, head_size)
    value_slots = value_part.reshape(context_count, block_rows, head_size)
    half_index = tensor_pos % per_kv
    key_total = key_slots[0]
    value_total = lax.dynamic_slice_in_dim(value_slots[0], half_index * half_size, half_size, 1)
    group_size = tensor_count * context_count
    for m in range(per_kv):
        for k in range(context_count):
            if m == 0 and k == 0:
                continue
            target_half = (tensor_pos ^ m) % per_kv
            term = jnp.concatenate(
                [
                    key_slots[k],
                    lax.dynamic_slice_in_dim(value_slots[k], target_half * half_size, half_size, 1),
                ],
                axis=1,
            )
            pairs = []
            for source in range(group_size):
                st, sc = divmod(source, context_count)
                pairs.append((source, (st ^ m) * context_count + (sc ^ k)))
            if m:
                term = term.astype(jnp.bfloat16)
            arrived = lax.ppermute(term, ("tensor", "context"), pairs).astype(jnp.float32)
            key_total = key_total + arrived[:, :head_size]
            value_total = value_total + arrived[:, head_size:]

    own_unit = key_unit[:block_rows]
    own_inverse = key_inverse[:block_rows]
    d_key_full = norm_backward(key_total, own_unit, own_inverse, k_gain)
    d_key_half = lax.dynamic_slice_in_dim(d_key_full, half_index * half_size, half_size, 1)
    d_key_out = with_layout_constraint(
        d_key_half.astype(jnp.bfloat16).reshape(1, 1, block_rows, half_size), OUT_LAYOUT
    )
    d_value_out = with_layout_constraint(
        value_total.astype(jnp.bfloat16).reshape(1, 1, block_rows, half_size), OUT_LAYOUT
    )
    return (
        d_query.reshape(1, 1, block_rows, head_count * head_size),
        d_key_out,
        d_value_out,
        gains[0],
        gains[1],
    )


def solution(mesh):
    placed = (
        P("dp", "context", None, "tensor"),
        P("dp", "context", None, None),
        P("dp", "context", None, None),
        P("dp", "context", "tensor", None),
        P("tensor", None),
        P(),
        P(),
        P("dp", None),
    )
    return jax.shard_map(
        shard_body,
        mesh=mesh,
        in_specs=placed,
        out_specs=(
            P("dp", "context", None, "tensor"),
            P("dp", "context", None, "tensor"),
            P("dp", "context", None, "tensor"),
            P(),
            P(),
        ),
        check_vma=False,
    )
```
